512 devices in a mesh: row: 32 (over z, core), col: 16 (over y, x).
Axes of the slice: x: 4, y: 4, z: 16, core: 2. Of those that a mesh axis runs over, the one named last changes fastest.
Arguments:
- pressure_in: float32 [1024, 256, 128], P('row', 'col'), may hold values from -6 to 6
- source: float32 [1024, 256, 128], P('row', 'col'), may hold values from -18 to 18
- permeability: float32 [1024, 256, 128], P('row', 'col'), may hold values from 0.2 to 5
Outputs:
- pressure_out: float32 [1024, 256, 128], P('row', 'col')
The draws below stay inside these ranges and needn't reach their ends.
All inputs are finite; a program needn't handle non-finite values.
Results may differ from the reference program's by a relative error of at most 0.0001.
Values sent between devices are 32-bit elements; how exact they have to be, the bound alone decides.
No kernel may reach another device: no remote copies, remote signals or barrier semaphores. Data moves between devices by JAX's collectives and lax.ppermute only.
A program may use at most 128 MiB of HBM per device.

```python
import math
import jax
import jax.numpy as jnp

NZ = 128
LEVELS = 3
NU1 = 2
NU2 = 2
CSWEEPS = 16
NX = 1024
NY = 256


def steps_of(own_key, dims, split, least, high):
    factor_of, own = 1.0, jax.random.fold_in(own_key, 6)
    for dim, shards_of in split:
        steps = jnp.exp(jax.random.uniform(jax.random.fold_in(own, dim), (shards_of,), jnp.float32, least / len(split), high / len(split)))
        factor_of = factor_of * jnp.repeat(steps, dims[dim] // shards_of).reshape([-1 if axis == dim else 1 for axis in range(len(dims))])
    return factor_of


def gaussian(stream_key, extent, deviation, bound, shards=(), kind=jnp.bfloat16):
    gain = steps_of(stream_key, extent, shards, -0.22, 0.18) if shards else 1.0
    values = jax.random.normal(stream_key, extent, jnp.float32) * deviation * gain
    return jnp.minimum(jnp.maximum(values, -bound), bound).astype(kind)


def setup_inputs(seed: int = 0) -> dict:
    keys = jax.random.split(jax.random.key(seed), 4)
    pressure_in = gaussian(keys[0], (NX, NY, NZ), 1.0, 6.0, ((0, 32), (1, 16)), jnp.float32)
    source = gaussian(keys[1], (NX, NY, NZ), 3.0, 18.0, ((0, 32), (1, 16)), jnp.float32)
    permeability = jnp.clip(jnp.exp(math.log(5.0) - 3.218876 * jax.random.uniform(keys[2], (NX, NY, NZ), jnp.float32) ** steps_of(keys[2], (NX, NY, NZ), ((0, 32), (1, 16)), -0.2, 0.2)), 0.2, 5.0)
    return dict(pressure_in=pressure_in, source=source, permeability=permeability)


OMEGA = 0.8


def harmonic(left, right, scale):
    return 2.0 * left * right / (left + right) * scale


def coefficients(padded, center, scale):
    west_x = harmonic(padded[:-2, 1:-1], center, scale)
    east_x = harmonic(center, padded[2:, 1:-1], scale)
    west_y = harmonic(padded[1:-1, :-2], center, scale)
    east_y = harmonic(center, padded[1:-1, 2:], scale)
    inner = harmonic(center[:, :, :-1], center[:, :, 1:], scale)
    below = jnp.concatenate([2.0 * center[:, :, :1] * scale, inner], axis=2)
    above = jnp.concatenate([inner, 2.0 * center[:, :, -1:] * scale], axis=2)
    diagonal = west_x + east_x + west_y + east_y + below + above
    return (west_x, east_x, west_y, east_y, below, above, diagonal)


def apply_operator(padded, center, faces):
    west_x, east_x, west_y, east_y, below, above, diagonal = faces
    zero_plane = jnp.zeros_like(center[:, :, :1])
    under = jnp.concatenate([zero_plane, center[:, :, :-1]], axis=2)
    over = jnp.concatenate([center[:, :, 1:], zero_plane], axis=2)
    beside_all = west_x * padded[:-2, 1:-1] + east_x * padded[2:, 1:-1]
    beside_all = beside_all + west_y * padded[1:-1, :-2] + east_y * padded[1:-1, 2:]
    beside_all = beside_all + below * under + above * over
    return diagonal * center - beside_all


def jacobi_sweep(pressure, right_side, faces, padder):
    return pressure + OMEGA * (right_side - apply_operator(padder(pressure), pressure, faces)) / faces[6]


def first_sweep(right_side, faces):
    return OMEGA * right_side / faces[6]


def coarsen(field):
    size_x, size_y, size_z = field.shape
    return field.reshape(size_x // 2, 2, size_y // 2, 2, size_z // 2, 2).mean(axis=(1, 3, 5))


def prolong(field):
    return jnp.repeat(jnp.repeat(jnp.repeat(field, 2, axis=0), 2, axis=1), 2, axis=2)


def wrap_pad(field):
    return jnp.pad(field, ((1, 1), (1, 1), (0, 0)), mode="wrap")


def reference(pressure_in, source, permeability):
    perms = [permeability]
    for depth_level in range(LEVELS):
        perms.append(coarsen(perms[-1]))
    all_faces = [coefficients(wrap_pad(perms[depth_level]), perms[depth_level], 0.25 ** depth_level) for depth_level in range(LEVELS + 1)]
    pressure = pressure_in
    right_side = source
    states = []
    for depth_level in range(LEVELS):
        faces = all_faces[depth_level]
        if depth_level == 0:
            for sweep_index in range(NU1):
                pressure = jacobi_sweep(pressure, right_side, faces, wrap_pad)
        else:
            pressure = first_sweep(right_side, faces)
            for sweep_index in range(NU1 - 1):
                pressure = jacobi_sweep(pressure, right_side, faces, wrap_pad)
        states.append((pressure, right_side))
        residual = right_side - apply_operator(wrap_pad(pressure), pressure, faces)
        right_side = coarsen(residual)
    faces = all_faces[LEVELS]
    correction = first_sweep(right_side, faces)
    for sweep_index in range(CSWEEPS - 1):
        correction = jacobi_sweep(correction, right_side, faces, wrap_pad)
    for depth_level in range(LEVELS - 1, -1, -1):
        pressure, right_side = states[depth_level]
        pressure = pressure + prolong(correction)
        for sweep_index in range(NU2):
            pressure = jacobi_sweep(pressure, right_side, all_faces[depth_level], wrap_pad)
        correction = pressure
    return correction
```

```python
import jax
import jax.numpy as jnp
from jax import lax
from jax.sharding import PartitionSpec as P

LEVELS = 3
NU1 = 2
NU2 = 2
CSWEEPS = 16

OMEGA = 0.8


def shift_from(x, axis, k):
    n = lax.axis_size(axis)
    return lax.ppermute(x, axis, [(i, (i + k) % n) for i in range(n)])


def halo(x, w):
    size_x = x.shape[-3]
    lower = shift_from(x[..., size_x - w :, :, :], "row", 1)
    upper = shift_from(x[..., :w, :, :], "row", -1)
    x = jnp.concatenate([lower, x, upper], axis=-3)
    size_y = x.shape[-2]
    lower = shift_from(x[..., :, size_y - w :, :], "col", 1)
    upper = shift_from(x[..., :, :w, :], "col", -1)
    return jnp.concatenate([lower, x, upper], axis=-2)


def trim(a, t, y=True):
    if t == 0:
        return a
    if y:
        return a[t:-t, t:-t]
    return a[t:-t]


def harmonic(left, right, scale):
    return 2.0 * left * right / (left + right) * scale


def faces_of(k, scale):
    c = k[1:-1, 1:-1]
    west_x = harmonic(k[:-2, 1:-1], c, scale)
    east_x = harmonic(c, k[2:, 1:-1], scale)
    west_y = harmonic(k[1:-1, :-2], c, scale)
    east_y = harmonic(c, k[1:-1, 2:], scale)
    inner = harmonic(c[:, :, :-1], c[:, :, 1:], scale)
    below = jnp.concatenate([2.0 * c[:, :, :1] * scale, inner], axis=2)
    above = jnp.concatenate([inner, 2.0 * c[:, :, -1:] * scale], axis=2)
    diagonal = west_x + east_x + west_y + east_y + below + above
    return (west_x, east_x, west_y, east_y, below, above, diagonal)


def apply_operator(v, faces):
    west_x, east_x, west_y, east_y, below, above, diagonal = faces
    c = v[1:-1, 1:-1]
    zero_plane = jnp.zeros_like(c[:, :, :1])
    under = jnp.concatenate([zero_plane, c[:, :, :-1]], axis=2)
    over = jnp.concatenate([c[:, :, 1:], zero_plane], axis=2)
    beside_all = west_x * v[:-2, 1:-1] + east_x * v[2:, 1:-1]
    beside_all = beside_all + west_y * v[1:-1, :-2] + east_y * v[1:-1, 2:]
    beside_all = beside_all + below * under + above * over
    return diagonal * c - beside_all


class Level:
    def __init__(self, faces, have, right_side, rhs_have):
        self.faces, self.have = faces, have
        self.right_side, self.rhs_have = right_side, rhs_have

    def faces_at(self, h, y=True):
        return tuple(trim(f, self.have - h, y) for f in self.faces)

    def rhs_at(self, h, y=True):
        return trim(self.right_side, self.rhs_have - h, y)

    def sweep(self, v, h):
        faces = self.faces_at(h)
        residual = self.rhs_at(h) - apply_operator(v, faces)
        return v[1:-1, 1:-1] + OMEGA * residual / faces[6]

    def first_sweep(self, h):
        return OMEGA * self.rhs_at(h) / self.faces_at(h)[6]

    def residual(self, v):
        return self.rhs_at(0) - apply_operator(v, self.faces_at(0))


def coarsen(field):
    size_x, size_y, size_z = field.shape
    t = field.reshape(size_x // 2, 2, size_y, size_z)
    t = t[:, 0] + t[:, 1]
    t = t[:, 0::2] + t[:, 1::2]
    t = t[:, :, 0::2] + t[:, :, 1::2]
    return t * 0.125


def prolong(field):
    return jnp.repeat(jnp.repeat(jnp.repeat(field, 2, axis=0), 2, axis=1), 2, axis=2)


def wrap_y(a):
    return jnp.concatenate([a[:, -1:], a, a[:, :1]], axis=1)


def coarse_solve(right_side, perm, scale):
    size_x, size_y, size_z = right_side.shape
    pair = jnp.stack([right_side, perm])
    band = lax.all_gather(pair, "col", axis=2, tiled=True)
    need = CSWEEPS + 1
    reach = -(-need // size_x)
    lower = [shift_from(band, "row", k) for k in range(reach, 0, -1)]
    upper = [shift_from(band, "row", -k) for k in range(1, reach + 1)]
    wide = jnp.concatenate(lower + [band] + upper, axis=1)
    cut = reach * size_x - need
    wide = wide[:, cut : wide.shape[1] - cut]
    rhs_band, perm_band = wide[0], wide[1]
    faces = faces_of(wrap_y(perm_band), scale)
    have = need - 1

    def faces_at(h):
        return tuple(trim(f, have - h, False) for f in faces)

    def rhs_at(h):
        return trim(rhs_band[1:-1], have - h, False)

    h = have
    v = OMEGA * rhs_at(h) / faces_at(h)[6]
    for _ in range(CSWEEPS - 1):
        h -= 1
        f = faces_at(h)
        residual = rhs_at(h) - apply_operator(wrap_y(v), f)
        v = v[1:-1] + OMEGA * residual / f[6]
    col = lax.axis_index("col")
    v = wrap_y(v)
    return lax.dynamic_slice_in_dim(v, col * size_y, size_y + 2, axis=1)


def on_device(pressure_in, source, permeability):
    scales = [0.25**level for level in range(LEVELS + 1)]
    k0, p0, b0 = halo(jnp.stack([permeability, pressure_in, source]), 4)
    lev0 = Level(faces_of(k0, scales[0]), 3, b0, 4)
    p = lev0.sweep(p0, 3)
    s0 = lev0.sweep(p, 2)
    rhs = coarsen(lev0.residual(trim(s0, 1)))
    perm = coarsen(permeability)
    k1, b1 = halo(jnp.stack([perm, rhs]), 5)
    lev1 = Level(faces_of(k1, scales[1]), 4, b1, 5)
    p = lev1.first_sweep(4)
    s1 = lev1.sweep(p, 3)
    rhs = coarsen(lev1.residual(trim(s1, 2)))
    perm = coarsen(perm)
    k2, b2 = halo(jnp.stack([perm, rhs]), 4)
    lev2 = Level(faces_of(k2, scales[2]), 3, b2, 4)
    p = lev2.first_sweep(3)
    s2 = lev2.sweep(p, 2)
    rhs = coarsen(lev2.residual(trim(s2, 1)))
    perm = coarsen(perm)
    correction = coarse_solve(rhs, perm, scales[3])
    q = s2 + prolong(correction)
    q = lev2.sweep(q, 1)
    u2 = lev2.sweep(q, 0)
    q = s1 + trim(prolong(halo(u2, 2)), 1)
    q = lev1.sweep(q, 2)
    u1 = lev1.sweep(q, 1)
    q = s0 + prolong(u1)
    q = lev0.sweep(q, 1)
    return lev0.sweep(q, 0)


def solution(mesh):
    placed = (P("row", "col", None), P("row", "col", None), P("row", "col", None))
    return jax.shard_map(
        on_device, mesh=mesh, in_specs=placed, out_specs=P("row", "col", None), check_vma=False
    )
```

```python
import jax
import jax.numpy as jnp
from jax import lax
from jax.sharding import PartitionSpec as P

LEVELS = 3
NU1 = 2
NU2 = 2
CSWEEPS = 16

OMEGA = 0.8


def shift_from(x, axis, k):
    n = lax.axis_size(axis)
    return lax.ppermute(x, axis, [(i, (i + k) % n) for i in range(n)])


def halo(x, w):
    size_x = x.shape[-3]
    lower = shift_from(x[..., size_x - w :, :, :], "row", 1)
    upper = shift_from(x[..., :w, :, :], "row", -1)
    x = jnp.concatenate([lower, x, upper], axis=-3)
    size_y = x.shape[-2]
    lower = shift_from(x[..., :, size_y - w :, :], "col", 1)
    upper = shift_from(x[..., :, :w, :], "col", -1)
    return jnp.concatenate([lower, x, upper], axis=-2)


def trim(a, t, y=True):
    if t == 0:
        return a
    if y:
        return a[t:-t, t:-t]
    return a[t:-t]


def harmonic(left, right, scale):
    return 2.0 * left * right / (left + right) * scale


def faces_of(k, scale):
    c = k[1:-1, 1:-1]
    west_x = harmonic(k[:-2, 1:-1], c, scale)
    east_x = harmonic(c, k[2:, 1:-1], scale)
    west_y = harmonic(k[1:-1, :-2], c, scale)
    east_y = harmonic(c, k[1:-1, 2:], scale)
    inner = harmonic(c[:, :, :-1], c[:, :, 1:], scale)
    below = jnp.concatenate([2.0 * c[:, :, :1] * scale, inner], axis=2)
    above = jnp.concatenate([inner, 2.0 * c[:, :, -1:] * scale], axis=2)
    diagonal = west_x + east_x + west_y + east_y + below + above
    return (west_x, east_x, west_y, east_y, below, above, diagonal)


def apply_operator(v, faces):
    west_x, east_x, west_y, east_y, below, above, diagonal = faces
    c = v[1:-1, 1:-1]
    zero_plane = jnp.zeros_like(c[:, :, :1])
    under = jnp.concatenate([zero_plane, c[:, :, :-1]], axis=2)
    over = jnp.concatenate([c[:, :, 1:], zero_plane], axis=2)
    beside_all = west_x * v[:-2, 1:-1] + east_x * v[2:, 1:-1]
    beside_all = beside_all + west_y * v[1:-1, :-2] + east_y * v[1:-1, 2:]
    beside_all = beside_all + below * under + above * over
    return diagonal * c - beside_all


class Level:
    def __init__(self, faces, have, right_side, rhs_have):
        self.faces, self.have = faces, have
        self.right_side, self.rhs_have = right_side, rhs_have

    def faces_at(self, h, y=True):
        return tuple(trim(f, self.have - h, y) for f in self.faces)

    def rhs_at(self, h, y=True):
        return trim(self.right_side, self.rhs_have - h, y)

    def sweep(self, v, h):
        faces = self.faces_at(h)
        residual = self.rhs_at(h) - apply_operator(v, faces)
        return v[1:-1, 1:-1] + OMEGA * residual / faces[6]

    def first_sweep(self, h):
        return OMEGA * self.rhs_at(h) / self.faces_at(h)[6]

    def residual(self, v):
        return self.rhs_at(0) - apply_operator(v, self.faces_at(0))


def coarsen(field):
    size_x, size_y, size_z = field.shape
    t = field.reshape(size_x // 2, 2, size_y, size_z)
    t = t[:, 0] + t[:, 1]
    t = t[:, 0::2] + t[:, 1::2]
    t = t[:, :, 0::2] + t[:, :, 1::2]
    return t * 0.125


def prolong(field):
    return jnp.repeat(jnp.repeat(jnp.repeat(field, 2, axis=0), 2, axis=1), 2, axis=2)


def wrap_y(a, w=1):
    return jnp.concatenate([a[:, -w:], a, a[:, :w]], axis=1)


class Band(Level):
    def faces_at(self, h, y=False):
        return super().faces_at(h, False)

    def rhs_at(self, h, y=False):
        return super().rhs_at(h, False)

    def sweep(self, v, h):
        faces = self.faces_at(h)
        residual = self.rhs_at(h) - apply_operator(wrap_y(v), faces)
        return v[1:-1] + OMEGA * residual / faces[6]

    def residual(self, v):
        return self.rhs_at(0) - apply_operator(wrap_y(v), self.faces_at(0))


def x_halo(x, w):
    size_x = x.shape[-3]
    lower = shift_from(x[..., size_x - w :, :, :], "row", 1)
    upper = shift_from(x[..., :w, :, :], "row", -1)
    return jnp.concatenate([lower, x, upper], axis=-3)


def rows_around(x, steps, axis):
    lower = [shift_from(x, "row", k) for k in reversed(steps)]
    upper = [shift_from(x, "row", -k) for k in steps]
    return jnp.concatenate(lower + [x] + upper, axis=axis)


def lane_roll(a, k):
    return jnp.roll(a, k, axis=-1)


def coarse_solve(right_side, perm, scale):
    size_x, size_y, size_z = right_side.shape
    lanes = size_y * size_z
    pair = jnp.stack([right_side, perm]).reshape(2, size_x, lanes)
    need = CSWEEPS + 1
    near = rows_around(pair, (1, 2), 1)
    wide = rows_around(near, (5,), 1)
    assert 7 * size_x >= need
    cut = 7 * size_x - need
    wide = wide[:, cut : wide.shape[1] - cut]
    rhs_band, k = wide[0, 1:-1], wide[1]
    lane = lax.broadcasted_iota(jnp.int32, (1, lanes), 1) % size_z
    first, last = lane == 0, lane == size_z - 1
    c = k[1:-1]
    west_x = harmonic(k[:-2], c, scale)
    east_x = harmonic(c, k[2:], scale)
    west_y = harmonic(lane_roll(c, size_z), c, scale)
    east_y = harmonic(c, lane_roll(c, -size_z), scale)
    below = jnp.where(first, 2.0 * c * scale, harmonic(lane_roll(c, 1), c, scale))
    above = jnp.where(last, 2.0 * c * scale, harmonic(c, lane_roll(c, -1), scale))
    diagonal = west_x + east_x + west_y + east_y + below + above

    def one_sweep(i, v):
        ext = jnp.concatenate([v[:1], v, v[-1:]], axis=0)
        under = jnp.where(first, 0.0, lane_roll(v, 1))
        over = jnp.where(last, 0.0, lane_roll(v, -1))
        beside_all = west_x * ext[:-2] + east_x * ext[2:]
        beside_all = beside_all + west_y * lane_roll(v, size_z) + east_y * lane_roll(v, -size_z)
        beside_all = beside_all + below * under + above * over
        return v + OMEGA * (rhs_band - (diagonal * v - beside_all)) / diagonal

    v = OMEGA * rhs_band / diagonal
    v = lax.fori_loop(1, CSWEEPS, one_sweep, v)
    have = need - 1 - (CSWEEPS - 1)
    drop = need - 1 - have
    v = v[drop : v.shape[0] - drop]
    return v.reshape(v.shape[0], size_y, size_z)


def on_device(pressure_in, source, permeability):
    scales = [0.25**level for level in range(LEVELS + 1)]
    k0, p0, b0 = halo(jnp.stack([permeability, pressure_in, source]), 4)
    lev0 = Level(faces_of(k0, scales[0]), 3, b0, 4)
    p = lev0.sweep(p0, 3)
    s0 = lev0.sweep(p, 2)
    rhs = coarsen(lev0.residual(trim(s0, 1)))
    perm = coarsen(permeability)
    k1, b1 = halo(jnp.stack([perm, rhs]), 5)
    lev1 = Level(faces_of(k1, scales[1]), 4, b1, 5)
    p = lev1.first_sweep(4)
    s1 = lev1.sweep(p, 3)
    rhs = coarsen(lev1.residual(trim(s1, 2)))
    perm = coarsen(perm)
    size_y2 = rhs.shape[1]
    band = lax.all_gather(jnp.stack([perm, rhs]), "col", axis=2, tiled=True)
    k2, b2 = x_halo(band, 4)
    lev2 = Band(faces_of(wrap_y(k2), scales[2]), 3, b2, 4)
    p = lev2.first_sweep(3)
    s2 = lev2.sweep(p, 2)
    rhs = coarsen(lev2.residual(s2[1:-1]))
    perm = coarsen(band[0])
    correction = coarse_solve(rhs, perm, scales[3])
    q = s2 + prolong(correction)
    q = lev2.sweep(q, 1)
    u2 = lev2.sweep(q, 0)
    u2 = wrap_y(x_halo(u2, 2), 2)
    col = lax.axis_index("col")
    u2 = lax.dynamic_slice_in_dim(u2, col * size_y2, size_y2 + 4, axis=1)
    q = s1 + trim(prolong(u2), 1)
    q = lev1.sweep(q, 2)
    u1 = lev1.sweep(q, 1)
    q = s0 + prolong(u1)
    q = lev0.sweep(q, 1)
    return lev0.sweep(q, 0)


def solution(mesh):
    placed = (P("row", "col", None), P("row", "col", None), P("row", "col", None))
    return jax.shard_map(
        on_device, mesh=mesh, in_specs=placed, out_specs=P("row", "col", None), check_vma=False
    )
```

```python
import jax
import jax.numpy as jnp
from jax import lax
from jax.sharding import PartitionSpec as P

LEVELS = 3
NU1 = 2
NU2 = 2
CSWEEPS = 16

OMEGA = 0.8


def shift_from(x, axis, k):
    n = lax.axis_size(axis)
    return lax.ppermute(x, axis, [(i, (i + k) % n) for i in range(n)])


def halo(x, w):
    size_x = x.shape[-3]
    lower = shift_from(x[..., size_x - w :, :, :], "row", 1)
    upper = shift_from(x[..., :w, :, :], "row", -1)
    x = jnp.concatenate([lower, x, upper], axis=-3)
    size_y = x.shape[-2]
    lower = shift_from(x[..., :, size_y - w :, :], "col", 1)
    upper = shift_from(x[..., :, :w, :], "col", -1)
    return jnp.concatenate([lower, x, upper], axis=-2)


def trim(a, t, y=True):
    if t == 0:
        return a
    if y:
        return a[t:-t, t:-t]
    return a[t:-t]


def harmonic(left, right, scale):
    return 2.0 * left * right / (left + right) * scale


def faces_of(k, scale):
    c = k[1:-1, 1:-1]
    west_x = harmonic(k[:-2, 1:-1], c, scale)
    east_x = harmonic(c, k[2:, 1:-1], scale)
    west_y = harmonic(k[1:-1, :-2], c, scale)
    east_y = harmonic(c, k[1:-1, 2:], scale)
    inner = harmonic(c[:, :, :-1], c[:, :, 1:], scale)
    below = jnp.concatenate([2.0 * c[:, :, :1] * scale, inner], axis=2)
    above = jnp.concatenate([inner, 2.0 * c[:, :, -1:] * scale], axis=2)
    diagonal = west_x + east_x + west_y + east_y + below + above
    return (west_x, east_x, west_y, east_y, below, above, diagonal)


def apply_operator(v, faces):
    west_x, east_x, west_y, east_y, below, above, diagonal = faces
    c = v[1:-1, 1:-1]
    zero_plane = jnp.zeros_like(c[:, :, :1])
    under = jnp.concatenate([zero_plane, c[:, :, :-1]], axis=2)
    over = jnp.concatenate([c[:, :, 1:], zero_plane], axis=2)
    beside_all = west_x * v[:-2, 1:-1] + east_x * v[2:, 1:-1]
    beside_all = beside_all + west_y * v[1:-1, :-2] + east_y * v[1:-1, 2:]
    beside_all = beside_all + below * under + above * over
    return diagonal * c - beside_all


class Level:
    def __init__(self, faces, have, right_side, rhs_have):
        self.faces, self.have = faces, have
        self.right_side, self.rhs_have = right_side, rhs_have

    def faces_at(self, h, y=True):
        return tuple(trim(f, self.have - h, y) for f in self.faces)

    def rhs_at(self, h, y=True):
        return trim(self.right_side, self.rhs_have - h, y)

    def sweep(self, v, h):
        faces = self.faces_at(h)
        residual = self.rhs_at(h) - apply_operator(v, faces)
        return v[1:-1, 1:-1] + OMEGA * residual / faces[6]

    def first_sweep(self, h):
        return OMEGA * self.rhs_at(h) / self.faces_at(h)[6]

    def residual(self, v):
        return self.rhs_at(0) - apply_operator(v, self.faces_at(0))


def pairs(n):
    i = lax.broadcasted_iota(jnp.int32, (n, n // 2), 0)
    j = lax.broadcasted_iota(jnp.int32, (n, n // 2), 1)
    return (i // 2 == j).astype(jnp.float32)


def along_z(field, matrix):
    size_x, size_y, size_z = field.shape
    flat = field.reshape(size_x * size_y, size_z)
    out = jnp.dot(flat, matrix, precision=lax.Precision.HIGHEST)
    return out.reshape(size_x, size_y, matrix.shape[1])


def along_y(field, matrix):
    size_x = field.shape[0]
    batched = jnp.broadcast_to(matrix, (size_x,) + matrix.shape)
    return jnp.einsum("xjy,xyz->xjz", batched, field, precision=lax.Precision.HIGHEST)


def coarsen(field):
    size_x, size_y, size_z = field.shape
    t = field.reshape(size_x // 2, 2, size_y, size_z)
    t = t[:, 0] + t[:, 1]
    t = along_z(t, pairs(size_z))
    t = along_y(t, pairs(size_y).T)
    return t * 0.125


def prolong(field):
    size_x, size_y, size_z = field.shape
    t = along_z(field, pairs(2 * size_z).T)
    t = along_y(t, pairs(2 * size_y))
    t = jnp.broadcast_to(t[:, None], (size_x, 2) + t.shape[1:])
    return t.reshape(2 * size_x, 2 * size_y, 2 * size_z)


def wrap_y(a, w=1):
    return jnp.concatenate([a[:, -w:], a, a[:, :w]], axis=1)


class Band(Level):
    def faces_at(self, h, y=False):
        return super().faces_at(h, False)

    def rhs_at(self, h, y=False):
        return super().rhs_at(h, False)

    def sweep(self, v, h):
        faces = self.faces_at(h)
        residual = self.rhs_at(h) - apply_operator(wrap_y(v), faces)
        return v[1:-1] + OMEGA * residual / faces[6]

    def residual(self, v):
        return self.rhs_at(0) - apply_operator(wrap_y(v), self.faces_at(0))


def x_halo(x, w):
    size_x = x.shape[-3]
    lower = shift_from(x[..., size_x - w :, :, :], "row", 1)
    upper = shift_from(x[..., :w, :, :], "row", -1)
    return jnp.concatenate([lower, x, upper], axis=-3)


def rows_around(x, steps, axis):
    lower = [shift_from(x, "row", k) for k in reversed(steps)]
    upper = [shift_from(x, "row", -k) for k in steps]
    return jnp.concatenate(lower + [x] + upper, axis=axis)


def lane_roll(a, k):
    return jnp.roll(a, k, axis=-1)


def coarse_solve(right_side, perm, scale):
    size_x, size_y, size_z = right_side.shape
    lanes = size_y * size_z
    pair = jnp.stack([right_side, perm]).reshape(2, size_x, lanes)
    need = CSWEEPS + 1
    near = rows_around(pair, (1, 2), 1)
    wide = rows_around(near, (5,), 1)
    assert 7 * size_x >= need
    cut = 7 * size_x - need
    wide = wide[:, cut : wide.shape[1] - cut]
    rhs_band, k = wide[0, 1:-1], wide[1]
    lane = lax.broadcasted_iota(jnp.int32, (1, lanes), 1) % size_z
    first, last = lane == 0, lane == size_z - 1
    c = k[1:-1]
    west_x = harmonic(k[:-2], c, scale)
    east_x = harmonic(c, k[2:], scale)
    west_y = harmonic(lane_roll(c, size_z), c, scale)
    east_y = harmonic(c, lane_roll(c, -size_z), scale)
    below = jnp.where(first, 2.0 * c * scale, harmonic(lane_roll(c, 1), c, scale))
    above = jnp.where(last, 2.0 * c * scale, harmonic(c, lane_roll(c, -1), scale))
    diagonal = west_x + east_x + west_y + east_y + below + above

    def one_sweep(i, v):
        ext = jnp.concatenate([v[:1], v, v[-1:]], axis=0)
        under = jnp.where(first, 0.0, lane_roll(v, 1))
        over = jnp.where(last, 0.0, lane_roll(v, -1))
        beside_all = west_x * ext[:-2] + east_x * ext[2:]
        beside_all = beside_all + west_y * lane_roll(v, size_z) + east_y * lane_roll(v, -size_z)
        beside_all = beside_all + below * under + above * over
        return v + OMEGA * (rhs_band - (diagonal * v - beside_all)) / diagonal

    v = OMEGA * rhs_band / diagonal
    v = lax.fori_loop(1, CSWEEPS, one_sweep, v)
    have = need - 1 - (CSWEEPS - 1)
    drop = need - 1 - have
    v = v[drop : v.shape[0] - drop]
    return v.reshape(v.shape[0], size_y, size_z)


def on_device(pressure_in, source, permeability):
    scales = [0.25**level for level in range(LEVELS + 1)]
    k0, p0, b0 = halo(jnp.stack([permeability, pressure_in, source]), 4)
    lev0 = Level(faces_of(k0, scales[0]), 3, b0, 4)
    p = lev0.sweep(p0, 3)
    s0 = lev0.sweep(p, 2)
    rhs = coarsen(lev0.residual(trim(s0, 1)))
    perm = coarsen(permeability)
    k1, b1 = halo(jnp.stack([perm, rhs]), 5)
    lev1 = Level(faces_of(k1, scales[1]), 4, b1, 5)
    p = lev1.first_sweep(4)
    s1 = lev1.sweep(p, 3)
    rhs = coarsen(lev1.residual(trim(s1, 2)))
    perm = coarsen(perm)
    size_y2 = rhs.shape[1]
    band = lax.all_gather(jnp.stack([perm, rhs]), "col", axis=2, tiled=True)
    k2, b2 = x_halo(band, 4)
    lev2 = Band(faces_of(wrap_y(k2), scales[2]), 3, b2, 4)
    p = lev2.first_sweep(3)
    s2 = lev2.sweep(p, 2)
    rhs = coarsen(lev2.residual(s2[1:-1]))
    perm = coarsen(band[0])
    correction = coarse_solve(rhs, perm, scales[3])
    q = s2 + prolong(correction)
    q = lev2.sweep(q, 1)
    u2 = lev2.sweep(q, 0)
    u2 = wrap_y(x_halo(u2, 2), 2)
    col = lax.axis_index("col")
    u2 = lax.dynamic_slice_in_dim(u2, col * size_y2, size_y2 + 4, axis=1)
    q = s1 + trim(prolong(u2), 1)
    q = lev1.sweep(q, 2)
    u1 = lev1.sweep(q, 1)
    q = s0 + prolong(u1)
    q = lev0.sweep(q, 1)
    return lev0.sweep(q, 0)


def solution(mesh):
    placed = (P("row", "col", None), P("row", "col", None), P("row", "col", None))
    return jax.shard_map(
        on_device, mesh=mesh, in_specs=placed, out_specs=P("row", "col", None), check_vma=False
    )
```

```python
import jax
import jax.numpy as jnp
from jax import lax
from jax.experimental import pallas as pl
from jax.experimental.pallas import tpu as pltpu
from jax.sharding import PartitionSpec as P

LEVELS = 3
NU1 = 2
NU2 = 2
CSWEEPS = 16

OMEGA = 0.8


def shift_from(x, axis, k):
    n = lax.axis_size(axis)
    return lax.ppermute(x, axis, [(i, (i + k) % n) for i in range(n)])


def halo(x, w):
    size_x = x.shape[-3]
    lower = shift_from(x[..., size_x - w :, :, :], "row", 1)
    upper = shift_from(x[..., :w, :, :], "row", -1)
    x = jnp.concatenate([lower, x, upper], axis=-3)
    size_y = x.shape[-2]
    lower = shift_from(x[..., :, size_y - w :, :], "col", 1)
    upper = shift_from(x[..., :, :w, :], "col", -1)
    return jnp.concatenate([lower, x, upper], axis=-2)


def trim(a, t, y=True):
    if t == 0:
        return a
    if y:
        return a[t:-t, t:-t]
    return a[t:-t]


def harmonic(left, right, scale):
    return 2.0 * left * right / (left + right) * scale


def faces_of(k, scale):
    c = k[1:-1, 1:-1]
    west_x = harmonic(k[:-2, 1:-1], c, scale)
    east_x = harmonic(c, k[2:, 1:-1], scale)
    west_y = harmonic(k[1:-1, :-2], c, scale)
    east_y = harmonic(c, k[1:-1, 2:], scale)
    inner = harmonic(c[:, :, :-1], c[:, :, 1:], scale)
    below = jnp.concatenate([2.0 * c[:, :, :1] * scale, inner], axis=2)
    above = jnp.concatenate([inner, 2.0 * c[:, :, -1:] * scale], axis=2)
    diagonal = west_x + east_x + west_y + east_y + below + above
    return (west_x, east_x, west_y, east_y, below, above, diagonal)


def apply_operator(v, faces):
    west_x, east_x, west_y, east_y, below, above, diagonal = faces
    c = v[1:-1, 1:-1]
    zero_plane = jnp.zeros_like(c[:, :, :1])
    under = jnp.concatenate([zero_plane, c[:, :, :-1]], axis=2)
    over = jnp.concatenate([c[:, :, 1:], zero_plane], axis=2)
    beside_all = west_x * v[:-2, 1:-1] + east_x * v[2:, 1:-1]
    beside_all = beside_all + west_y * v[1:-1, :-2] + east_y * v[1:-1, 2:]
    beside_all = beside_all + below * under + above * over
    return diagonal * c - beside_all


class Level:
    def __init__(self, faces, have, right_side, rhs_have):
        self.faces, self.have = faces, have
        self.right_side, self.rhs_have = right_side, rhs_have

    def faces_at(self, h, y=True):
        return tuple(trim(f, self.have - h, y) for f in self.faces)

    def rhs_at(self, h, y=True):
        return trim(self.right_side, self.rhs_have - h, y)

    def sweep(self, v, h):
        faces = self.faces_at(h)
        residual = self.rhs_at(h) - apply_operator(v, faces)
        return v[1:-1, 1:-1] + OMEGA * residual / faces[6]

    def first_sweep(self, h):
        return OMEGA * self.rhs_at(h) / self.faces_at(h)[6]

    def residual(self, v):
        return self.rhs_at(0) - apply_operator(v, self.faces_at(0))


def pairs(n):
    i = lax.broadcasted_iota(jnp.int32, (n, n // 2), 0)
    j = lax.broadcasted_iota(jnp.int32, (n, n // 2), 1)
    return (i // 2 == j).astype(jnp.float32)


def along_z(field, matrix):
    size_x, size_y, size_z = field.shape
    flat = field.reshape(size_x * size_y, size_z)
    out = jnp.dot(flat, matrix, precision=lax.Precision.HIGHEST)
    return out.reshape(size_x, size_y, matrix.shape[1])


def along_y(field, matrix):
    size_x = field.shape[0]
    batched = jnp.broadcast_to(matrix, (size_x,) + matrix.shape)
    return jnp.einsum("xjy,xyz->xjz", batched, field, precision=lax.Precision.HIGHEST)


def coarsen(field):
    size_x, size_y, size_z = field.shape
    t = field.reshape(size_x // 2, 2, size_y, size_z)
    t = t[:, 0] + t[:, 1]
    t = along_z(t, pairs(size_z))
    t = along_y(t, pairs(size_y).T)
    return t * 0.125


def prolong(field):
    size_x, size_y, size_z = field.shape
    t = along_z(field, pairs(2 * size_z).T)
    t = along_y(t, pairs(2 * size_y))
    t = jnp.broadcast_to(t[:, None], (size_x, 2) + t.shape[1:])
    return t.reshape(2 * size_x, 2 * size_y, 2 * size_z)


def wrap_y(a, w=1):
    return jnp.concatenate([a[:, -w:], a, a[:, :w]], axis=1)


class Band(Level):
    def faces_at(self, h, y=False):
        return super().faces_at(h, False)

    def rhs_at(self, h, y=False):
        return super().rhs_at(h, False)

    def sweep(self, v, h):
        faces = self.faces_at(h)
        residual = self.rhs_at(h) - apply_operator(wrap_y(v), faces)
        return v[1:-1] + OMEGA * residual / faces[6]

    def residual(self, v):
        return self.rhs_at(0) - apply_operator(wrap_y(v), self.faces_at(0))


def x_halo(x, w):
    size_x = x.shape[-3]
    lower = shift_from(x[..., size_x - w :, :, :], "row", 1)
    upper = shift_from(x[..., :w, :, :], "row", -1)
    return jnp.concatenate([lower, x, upper], axis=-3)


def rows_around(x, steps, axis):
    lower = [shift_from(x, "row", k) for k in reversed(steps)]
    upper = [shift_from(x, "row", -k) for k in steps]
    return jnp.concatenate(lower + [x] + upper, axis=axis)


def coarse_kernel(scale, size_z, k_ref, b_ref, out_ref):
    k = k_ref[...]
    b = b_ref[...]
    rows, lanes = k.shape
    lane = lax.broadcasted_iota(jnp.int32, (rows, lanes), 1) % size_z
    first, last = lane == 0, lane == size_z - 1

    def x_lower(a):
        return pltpu.roll(a, 1, 0)

    def x_upper(a):
        return pltpu.roll(a, rows - 1, 0)

    def y_lower(a):
        return pltpu.roll(a, size_z, 1)

    def y_upper(a):
        return pltpu.roll(a, lanes - size_z, 1)

    def z_lower(a):
        return pltpu.roll(a, 1, 1)

    def z_upper(a):
        return pltpu.roll(a, lanes - 1, 1)

    west_x = harmonic(x_lower(k), k, scale)
    east_x = harmonic(k, x_upper(k), scale)
    west_y = harmonic(y_lower(k), k, scale)
    east_y = harmonic(k, y_upper(k), scale)
    below = jnp.where(first, 2.0 * k * scale, harmonic(z_lower(k), k, scale))
    above = jnp.where(last, 2.0 * k * scale, harmonic(k, z_upper(k), scale))
    diagonal = west_x + east_x + west_y + east_y + below + above

    def one_sweep(i, v):
        under = jnp.where(first, 0.0, z_lower(v))
        over = jnp.where(last, 0.0, z_upper(v))
        beside_all = west_x * x_lower(v) + east_x * x_upper(v)
        beside_all = beside_all + west_y * y_lower(v) + east_y * y_upper(v)
        beside_all = beside_all + below * under + above * over
        return v + OMEGA * (b - (diagonal * v - beside_all)) / diagonal

    v = OMEGA * b / diagonal
    out_ref[...] = lax.fori_loop(1, CSWEEPS, one_sweep, v)


def coarse_solve(right_side, perm, scale):
    size_x, size_y, size_z = right_side.shape
    lanes = size_y * size_z
    pair = jnp.stack([right_side, perm]).reshape(2, size_x, lanes)
    near = rows_around(pair, (1, 2), 1)
    wide = rows_around(near, (5,), 1)
    keep = CSWEEPS + 2
    keep += (-(size_x + 2 * keep)) % 8 // 2
    cut = 7 * size_x - keep
    assert cut >= 0
    wide = wide[:, cut : wide.shape[1] - cut]
    rows = wide.shape[1]
    call = pl.pallas_call(
        lambda k_ref, b_ref, out_ref: coarse_kernel(scale, size_z, k_ref, b_ref, out_ref),
        out_shape=jax.ShapeDtypeStruct((rows, lanes), jnp.float32),
        cost_estimate=pl.CostEstimate(
            flops=40 * CSWEEPS * rows * lanes, transcendentals=0, bytes_accessed=12 * rows * lanes
        ),
    )
    v = call(wide[1], wide[0])
    drop = keep - 1
    v = v[drop : rows - drop]
    return v.reshape(v.shape[0], size_y, size_z)


def on_device(pressure_in, source, permeability):
    scales = [0.25**level for level in range(LEVELS + 1)]
    k0, p0, b0 = halo(jnp.stack([permeability, pressure_in, source]), 4)
    lev0 = Level(faces_of(k0, scales[0]), 3, b0, 4)
    p = lev0.sweep(p0, 3)
    s0 = lev0.sweep(p, 2)
    rhs = coarsen(lev0.residual(trim(s0, 1)))
    perm = coarsen(permeability)
    k1, b1 = halo(jnp.stack([perm, rhs]), 5)
    lev1 = Level(faces_of(k1, scales[1]), 4, b1, 5)
    p = lev1.first_sweep(4)
    s1 = lev1.sweep(p, 3)
    rhs = coarsen(lev1.residual(trim(s1, 2)))
    perm = coarsen(perm)
    size_y2 = rhs.shape[1]
    band = lax.all_gather(jnp.stack([perm, rhs]), "col", axis=2, tiled=True)
    k2, b2 = x_halo(band, 4)
    lev2 = Band(faces_of(wrap_y(k2), scales[2]), 3, b2, 4)
    p = lev2.first_sweep(3)
    s2 = lev2.sweep(p, 2)
    rhs = coarsen(lev2.residual(s2[1:-1]))
    perm = coarsen(band[0])
    correction = coarse_solve(rhs, perm, scales[3])
    q = s2 + prolong(correction)
    q = lev2.sweep(q, 1)
    u2 = lev2.sweep(q, 0)
    u2 = wrap_y(x_halo(u2, 2), 2)
    col = lax.axis_index("col")
    u2 = lax.dynamic_slice_in_dim(u2, col * size_y2, size_y2 + 4, axis=1)
    q = s1 + trim(prolong(u2), 1)
    q = lev1.sweep(q, 2)
    u1 = lev1.sweep(q, 1)
    q = s0 + prolong(u1)
    q = lev0.sweep(q, 1)
    return lev0.sweep(q, 0)


def solution(mesh):
    placed = (P("row", "col", None), P("row", "col", None), P("row", "col", None))
    return jax.shard_map(
        on_device, mesh=mesh, in_specs=placed, out_specs=P("row", "col", None), check_vma=False
    )
```

```python
import jax
import jax.numpy as jnp
from jax import lax
from jax.experimental import pallas as pl
from jax.experimental.pallas import tpu as pltpu
from jax.sharding import PartitionSpec as P

LEVELS = 3
NU1 = 2
NU2 = 2
CSWEEPS = 16

OMEGA = 0.8


def shift_from(x, axis, k):
    n = lax.axis_size(axis)
    return lax.ppermute(x, axis, [(i, (i + k) % n) for i in range(n)])


def halo(x, w):
    size_x = x.shape[-3]
    lower = shift_from(x[..., size_x - w :, :, :], "row", 1)
    upper = shift_from(x[..., :w, :, :], "row", -1)
    x = jnp.concatenate([lower, x, upper], axis=-3)
    size_y = x.shape[-2]
    lower = shift_from(x[..., :, size_y - w :, :], "col", 1)
    upper = shift_from(x[..., :, :w, :], "col", -1)
    return jnp.concatenate([lower, x, upper], axis=-2)


def trim(a, t, y=True):
    if t == 0:
        return a
    if y:
        return a[t:-t, t:-t]
    return a[t:-t]


def harmonic(left, right, scale):
    return 2.0 * left * right / (left + right) * scale


def faces_of(k, scale):
    c = k[1:-1, 1:-1]
    west_x = harmonic(k[:-2, 1:-1], c, scale)
    east_x = harmonic(c, k[2:, 1:-1], scale)
    west_y = harmonic(k[1:-1, :-2], c, scale)
    east_y = harmonic(c, k[1:-1, 2:], scale)
    inner = harmonic(c[:, :, :-1], c[:, :, 1:], scale)
    below = jnp.concatenate([2.0 * c[:, :, :1] * scale, inner], axis=2)
    above = jnp.concatenate([inner, 2.0 * c[:, :, -1:] * scale], axis=2)
    diagonal = west_x + east_x + west_y + east_y + below + above
    return (west_x, east_x, west_y, east_y, below, above, diagonal)


def apply_operator(v, faces):
    west_x, east_x, west_y, east_y, below, above, diagonal = faces
    c = v[1:-1, 1:-1]
    zero_plane = jnp.zeros_like(c[:, :, :1])
    under = jnp.concatenate([zero_plane, c[:, :, :-1]], axis=2)
    over = jnp.concatenate([c[:, :, 1:], zero_plane], axis=2)
    beside_all = west_x * v[:-2, 1:-1] + east_x * v[2:, 1:-1]
    beside_all = beside_all + west_y * v[1:-1, :-2] + east_y * v[1:-1, 2:]
    beside_all = beside_all + below * under + above * over
    return diagonal * c - beside_all


class Level:
    def __init__(self, faces, have, right_side, rhs_have):
        self.faces, self.have = faces, have
        self.right_side, self.rhs_have = right_side, rhs_have

    def faces_at(self, h, y=True):
        return tuple(trim(f, self.have - h, y) for f in self.faces)

    def rhs_at(self, h, y=True):
        return trim(self.right_side, self.rhs_have - h, y)

    def sweep(self, v, h):
        faces = self.faces_at(h)
        residual = self.rhs_at(h) - apply_operator(v, faces)
        return v[1:-1, 1:-1] + OMEGA * residual / faces[6]

    def first_sweep(self, h):
        return OMEGA * self.rhs_at(h) / self.faces_at(h)[6]

    def residual(self, v):
        return self.rhs_at(0) - apply_operator(v, self.faces_at(0))


def pairs(n):
    i = lax.broadcasted_iota(jnp.int32, (n, n // 2), 0)
    j = lax.broadcasted_iota(jnp.int32, (n, n // 2), 1)
    return (i // 2 == j).astype(jnp.float32)


def along_z(field, matrix):
    size_x, size_y, size_z = field.shape
    flat = field.reshape(size_x * size_y, size_z)
    out = jnp.dot(flat, matrix, precision=lax.Precision.HIGHEST)
    return out.reshape(size_x, size_y, matrix.shape[1])


def along_y(field, matrix):
    size_x = field.shape[0]
    batched = jnp.broadcast_to(matrix, (size_x,) + matrix.shape)
    return jnp.einsum("xjy,xyz->xjz", batched, field, precision=lax.Precision.HIGHEST)


def coarsen(field):
    size_x, size_y, size_z = field.shape
    t = field.reshape(size_x // 2, 2, size_y, size_z)
    t = t[:, 0] + t[:, 1]
    t = along_z(t, pairs(size_z))
    t = along_y(t, pairs(size_y).T)
    return t * 0.125


def prolong(field):
    size_x, size_y, size_z = field.shape
    t = along_z(field, pairs(2 * size_z).T)
    t = along_y(t, pairs(2 * size_y))
    t = jnp.broadcast_to(t[:, None], (size_x, 2) + t.shape[1:])
    return t.reshape(2 * size_x, 2 * size_y, 2 * size_z)


def wrap_y(a, w=1):
    return jnp.concatenate([a[:, -w:], a, a[:, :w]], axis=1)


class Band(Level):
    def faces_at(self, h, y=False):
        return super().faces_at(h, False)

    def rhs_at(self, h, y=False):
        return super().rhs_at(h, False)

    def sweep(self, v, h):
        faces = self.faces_at(h)
        residual = self.rhs_at(h) - apply_operator(wrap_y(v), faces)
        return v[1:-1] + OMEGA * residual / faces[6]

    def residual(self, v):
        return self.rhs_at(0) - apply_operator(wrap_y(v), self.faces_at(0))


def x_halo(x, w):
    size_x = x.shape[-3]
    lower = shift_from(x[..., size_x - w :, :, :], "row", 1)
    upper = shift_from(x[..., :w, :, :], "row", -1)
    return jnp.concatenate([lower, x, upper], axis=-3)


def rows_around(x, steps, axis):
    lower = [shift_from(x, "row", k) for k in reversed(steps)]
    upper = [shift_from(x, "row", -k) for k in steps]
    return jnp.concatenate(lower + [x] + upper, axis=axis)


def coarse_kernel(scale, size_z, spans, keep, lower_ref, own_ref, upper_ref, out_ref, tile_ref):
    span, extra = spans
    for f in range(2):
        tile_ref[f, 0:extra] = lower_ref[f, span - extra : span]
        tile_ref[f, extra : extra + span] = own_ref[f]
        tile_ref[f, extra + span : 2 * extra + span] = upper_ref[f, 0:extra]
    b = tile_ref[0]
    k = tile_ref[1]
    rows, lanes = k.shape
    lane = lax.broadcasted_iota(jnp.int32, (rows, lanes), 1) % size_z
    first, last = lane == 0, lane == size_z - 1

    def x_lower(a):
        return pltpu.roll(a, 1, 0)

    def x_upper(a):
        return pltpu.roll(a, rows - 1, 0)

    def y_lower(a):
        return pltpu.roll(a, size_z, 1)

    def y_upper(a):
        return pltpu.roll(a, lanes - size_z, 1)

    def z_lower(a):
        return pltpu.roll(a, 1, 1)

    def z_upper(a):
        return pltpu.roll(a, lanes - 1, 1)

    west_x = harmonic(x_lower(k), k, scale)
    east_x = harmonic(k, x_upper(k), scale)
    west_y = harmonic(y_lower(k), k, scale)
    east_y = harmonic(k, y_upper(k), scale)
    below = jnp.where(first, 2.0 * k * scale, harmonic(z_lower(k), k, scale))
    above = jnp.where(last, 2.0 * k * scale, harmonic(k, z_upper(k), scale))
    diagonal = west_x + east_x + west_y + east_y + below + above

    def one_sweep(i, v):
        under = jnp.where(first, 0.0, z_lower(v))
        over = jnp.where(last, 0.0, z_upper(v))
        beside_all = west_x * x_lower(v) + east_x * x_upper(v)
        beside_all = beside_all + west_y * y_lower(v) + east_y * y_upper(v)
        beside_all = beside_all + below * under + above * over
        return v + OMEGA * (b - (diagonal * v - beside_all)) / diagonal

    v = OMEGA * b / diagonal
    v = lax.fori_loop(1, CSWEEPS, one_sweep, v)
    out_ref[...] = v[(rows - keep) // 2 : (rows + keep) // 2]


def coarse_solve(right_side, perm, scale):
    size_x, size_y, size_z = right_side.shape
    lanes = size_y * size_z
    pair = jnp.stack([right_side, perm]).reshape(2, size_x, lanes)
    near = rows_around(pair, (1, 2), 1)
    span = near.shape[1]
    extra = CSWEEPS + 2 - (span - size_x) // 2
    extra += (-(span + 2 * extra)) % 8 // 2
    assert 0 < extra <= span
    rows = span + 2 * extra
    keep = 8
    assert (rows - keep) // 2 >= CSWEEPS
    lower, upper = shift_from(near, "row", 5), shift_from(near, "row", -5)
    call = pl.pallas_call(
        lambda *refs: coarse_kernel(scale, size_z, (span, extra), keep, *refs),
        out_shape=jax.ShapeDtypeStruct((keep, lanes), jnp.float32),
        scratch_shapes=[pltpu.VMEM((2, rows, lanes), jnp.float32)],
        cost_estimate=pl.CostEstimate(
            flops=40 * CSWEEPS * rows * lanes, transcendentals=0, bytes_accessed=24 * rows * lanes
        ),
    )
    v = call(lower, near, upper)
    return v.reshape(keep, size_y, size_z)


def on_device(pressure_in, source, permeability):
    scales = [0.25**level for level in range(LEVELS + 1)]
    k0, p0, b0 = halo(jnp.stack([permeability, pressure_in, source]), 4)
    lev0 = Level(faces_of(k0, scales[0]), 3, b0, 4)
    p = lev0.sweep(p0, 3)
    s0 = lev0.sweep(p, 2)
    rhs = coarsen(lev0.residual(trim(s0, 1)))
    perm = coarsen(permeability)
    k1, b1 = halo(jnp.stack([perm, rhs]), 5)
    lev1 = Level(faces_of(k1, scales[1]), 4, b1, 5)
    p = lev1.first_sweep(4)
    s1 = lev1.sweep(p, 3)
    rhs = coarsen(lev1.residual(trim(s1, 2)))
    perm = coarsen(perm)
    size_y2 = rhs.shape[1]
    band = lax.all_gather(jnp.stack([perm, rhs]), "col", axis=2, tiled=True)
    k2, b2 = x_halo(band, 4)
    lev2 = Band(faces_of(wrap_y(k2), scales[2]), 3, b2, 4)
    p = lev2.first_sweep(3)
    s2 = lev2.sweep(p, 2)
    rhs = coarsen(lev2.residual(s2[1:-1]))
    perm = coarsen(band[0])
    correction = coarse_solve(rhs, perm, scales[3])
    q = s2 + prolong(correction)[2:-2]
    q = lev2.sweep(q, 1)
    u2 = lev2.sweep(q, 0)
    u2 = wrap_y(x_halo(u2, 2), 2)
    col = lax.axis_index("col")
    u2 = lax.dynamic_slice_in_dim(u2, col * size_y2, size_y2 + 4, axis=1)
    q = s1 + trim(prolong(u2), 1)
    q = lev1.sweep(q, 2)
    u1 = lev1.sweep(q, 1)
    q = s0 + prolong(u1)
    q = lev0.sweep(q, 1)
    return lev0.sweep(q, 0)


def solution(mesh):
    placed = (P("row", "col", None), P("row", "col", None), P("row", "col", None))
    return jax.shard_map(
        on_device, mesh=mesh, in_specs=placed, out_specs=P("row", "col", None), check_vma=False
    )
```

```python
import jax
import jax.numpy as jnp
from jax import lax
from jax.experimental import pallas as pl
from jax.experimental.pallas import tpu as pltpu
from jax.sharding import PartitionSpec as P

LEVELS = 3
NU1 = 2
NU2 = 2
CSWEEPS = 16

OMEGA = 0.8


def shift_from(x, axis, k):
    n = lax.axis_size(axis)
    return lax.ppermute(x, axis, [(i, (i + k) % n) for i in range(n)])


def halo(x, w):
    wx, wy = w
    size_x = x.shape[-3]
    lower = shift_from(x[..., size_x - wx :, :, :], "row", 1)
    upper = shift_from(x[..., :wx, :, :], "row", -1)
    x = jnp.concatenate([lower, x, upper], axis=-3)
    size_y = x.shape[-2]
    lower = shift_from(x[..., :, size_y - wy :, :], "col", 1)
    upper = shift_from(x[..., :, :wy, :], "col", -1)
    return jnp.concatenate([lower, x, upper], axis=-2)


def trim(a, t):
    tx, ty = t if isinstance(t, tuple) else (t, 0)
    return a[tx : a.shape[0] - tx, ty : a.shape[1] - ty]


def less(a, b):
    return tuple(i - j for i, j in zip(a, b))


def more(a, k):
    return tuple(i + k for i in a)


def harmonic(left, right, scale):
    return 2.0 * left * right / (left + right) * scale


def faces_of(k, scale):
    c = k[1:-1, 1:-1]
    west_x = harmonic(k[:-2, 1:-1], c, scale)
    east_x = harmonic(c, k[2:, 1:-1], scale)
    west_y = harmonic(k[1:-1, :-2], c, scale)
    east_y = harmonic(c, k[1:-1, 2:], scale)
    inner = harmonic(c[:, :, :-1], c[:, :, 1:], scale)
    below = jnp.concatenate([2.0 * c[:, :, :1] * scale, inner], axis=2)
    above = jnp.concatenate([inner, 2.0 * c[:, :, -1:] * scale], axis=2)
    diagonal = west_x + east_x + west_y + east_y + below + above
    return (west_x, east_x, west_y, east_y, below, above, diagonal)


def apply_operator(v, faces):
    west_x, east_x, west_y, east_y, below, above, diagonal = faces
    c = v[1:-1, 1:-1]
    zero_plane = jnp.zeros_like(c[:, :, :1])
    under = jnp.concatenate([zero_plane, c[:, :, :-1]], axis=2)
    over = jnp.concatenate([c[:, :, 1:], zero_plane], axis=2)
    beside_all = west_x * v[:-2, 1:-1] + east_x * v[2:, 1:-1]
    beside_all = beside_all + west_y * v[1:-1, :-2] + east_y * v[1:-1, 2:]
    beside_all = beside_all + below * under + above * over
    return diagonal * c - beside_all


class Level:
    def __init__(self, faces, have, right_side, rhs_have):
        self.faces, self.have = faces, have
        self.right_side, self.rhs_have = right_side, rhs_have

    def faces_at(self, h):
        return tuple(trim(f, less(self.have, h)) for f in self.faces)

    def rhs_at(self, h):
        return trim(self.right_side, less(self.rhs_have, h))

    def sweep(self, v, h):
        faces = self.faces_at(h)
        residual = self.rhs_at(h) - apply_operator(v, faces)
        return v[1:-1, 1:-1] + OMEGA * residual / faces[6]

    def first_sweep(self, h):
        return OMEGA * self.rhs_at(h) / self.faces_at(h)[6]

    def residual(self, v, h):
        return self.rhs_at(h) - apply_operator(v, self.faces_at(h))


def pairs(n):
    i = lax.broadcasted_iota(jnp.int32, (n, n // 2), 0)
    j = lax.broadcasted_iota(jnp.int32, (n, n // 2), 1)
    return (i // 2 == j).astype(jnp.float32)


def along_z(field, matrix):
    size_x, size_y, size_z = field.shape
    flat = field.reshape(size_x * size_y, size_z)
    out = jnp.dot(flat, matrix, precision=lax.Precision.HIGHEST)
    return out.reshape(size_x, size_y, matrix.shape[1])


def along_y(field, matrix):
    size_x = field.shape[0]
    batched = jnp.broadcast_to(matrix, (size_x,) + matrix.shape)
    return jnp.einsum("xjy,xyz->xjz", batched, field, precision=lax.Precision.HIGHEST)


def coarsen(field):
    size_x, size_y, size_z = field.shape
    t = field.reshape(size_x // 2, 2, size_y, size_z)
    t = t[:, 0] + t[:, 1]
    t = along_z(t, pairs(size_z))
    t = along_y(t, pairs(size_y).T)
    return t * 0.125


def prolong(field):
    size_x, size_y, size_z = field.shape
    t = along_z(field, pairs(2 * size_z).T)
    t = along_y(t, pairs(2 * size_y))
    t = jnp.broadcast_to(t[:, None], (size_x, 2) + t.shape[1:])
    return t.reshape(2 * size_x, 2 * size_y, 2 * size_z)


def wrap_y(a, w=1):
    return jnp.concatenate([a[:, -w:], a, a[:, :w]], axis=1)


class Band:
    def __init__(self, faces, have, right_side, rhs_have):
        self.faces, self.have = faces, have
        self.right_side, self.rhs_have = right_side, rhs_have

    def faces_at(self, h):
        return tuple(trim(f, self.have - h) for f in self.faces)

    def rhs_at(self, h):
        return trim(self.right_side, self.rhs_have - h)

    def sweep(self, v, h):
        faces = self.faces_at(h)
        residual = self.rhs_at(h) - apply_operator(wrap_y(v), faces)
        return v[1:-1] + OMEGA * residual / faces[6]

    def first_sweep(self, h):
        return OMEGA * self.rhs_at(h) / self.faces_at(h)[6]

    def residual(self, v):
        return self.rhs_at(0) - apply_operator(wrap_y(v), self.faces_at(0))


def rows_around(x, steps, axis):
    lower = [shift_from(x, "row", k) for k in reversed(steps)]
    upper = [shift_from(x, "row", -k) for k in steps]
    return jnp.concatenate(lower + [x] + upper, axis=axis)


def coarse_kernel(scale, size_z, spans, keep, lower_ref, own_ref, upper_ref, out_ref, tile_ref):
    span, extra = spans
    for f in range(2):
        tile_ref[f, 0:extra] = lower_ref[f, span - extra : span]
        tile_ref[f, extra : extra + span] = own_ref[f]
        tile_ref[f, extra + span : 2 * extra + span] = upper_ref[f, 0:extra]
    b = tile_ref[0]
    k = tile_ref[1]
    rows, lanes = k.shape
    lane = lax.broadcasted_iota(jnp.int32, (rows, lanes), 1) % size_z
    first, last = lane == 0, lane == size_z - 1

    def x_lower(a):
        return pltpu.roll(a, 1, 0)

    def x_upper(a):
        return pltpu.roll(a, rows - 1, 0)

    def y_lower(a):
        return pltpu.roll(a, size_z, 1)

    def y_upper(a):
        return pltpu.roll(a, lanes - size_z, 1)

    def z_lower(a):
        return pltpu.roll(a, 1, 1)

    def z_upper(a):
        return pltpu.roll(a, lanes - 1, 1)

    west_x = harmonic(x_lower(k), k, scale)
    east_x = harmonic(k, x_upper(k), scale)
    west_y = harmonic(y_lower(k), k, scale)
    east_y = harmonic(k, y_upper(k), scale)
    below = jnp.where(first, 2.0 * k * scale, harmonic(z_lower(k), k, scale))
    above = jnp.where(last, 2.0 * k * scale, harmonic(k, z_upper(k), scale))
    diagonal = west_x + east_x + west_y + east_y + below + above

    def one_sweep(i, v):
        under = jnp.where(first, 0.0, z_lower(v))
        over = jnp.where(last, 0.0, z_upper(v))
        beside_all = west_x * x_lower(v) + east_x * x_upper(v)
        beside_all = beside_all + west_y * y_lower(v) + east_y * y_upper(v)
        beside_all = beside_all + below * under + above * over
        return v + OMEGA * (b - (diagonal * v - beside_all)) / diagonal

    v = OMEGA * b / diagonal
    v = lax.fori_loop(1, CSWEEPS, one_sweep, v)
    out_ref[...] = v[(rows - keep) // 2 : (rows + keep) // 2]


def coarse_solve(right_side, perm, scale):
    size_x, size_y, size_z = right_side.shape
    lanes = size_y * size_z
    pair = jnp.stack([right_side, perm]).reshape(2, size_x, lanes)
    near = rows_around(pair, (1, 2), 1)
    span = near.shape[1]
    extra = CSWEEPS + 2 - (span - size_x) // 2
    extra += (-(span + 2 * extra)) % 8 // 2
    assert 0 < extra <= span
    rows = span + 2 * extra
    keep = 8
    assert (rows - keep) // 2 >= CSWEEPS
    lower, upper = shift_from(near, "row", 5), shift_from(near, "row", -5)
    call = pl.pallas_call(
        lambda *refs: coarse_kernel(scale, size_z, (span, extra), keep, *refs),
        out_shape=jax.ShapeDtypeStruct((keep, lanes), jnp.float32),
        scratch_shapes=[pltpu.VMEM((2, rows, lanes), jnp.float32)],
        cost_estimate=pl.CostEstimate(
            flops=40 * CSWEEPS * rows * lanes, transcendentals=0, bytes_accessed=24 * rows * lanes
        ),
    )
    v = call(lower, near, upper)
    return v.reshape(keep, size_y, size_z)


def on_device(pressure_in, source, permeability):
    scales = [0.25**level for level in range(LEVELS + 1)]
    k0, p0, b0 = halo(jnp.stack([permeability, pressure_in, source]), (4, 4))
    lev0 = Level(faces_of(k0, scales[0]), (3, 3), b0, (4, 4))
    p = lev0.sweep(p0, (3, 3))
    s0 = lev0.sweep(p, (2, 2))
    rhs = coarsen(lev0.residual(trim(s0, (1, 1)), (0, 0)))
    perm = coarsen(permeability)
    k1, b1 = halo(jnp.stack([perm, rhs]), (13, 5))
    lev1 = Level(faces_of(k1, scales[1]), (12, 4), b1, (13, 5))
    p = lev1.first_sweep((12, 4))
    s1 = lev1.sweep(p, (11, 3))
    rhs = coarsen(lev1.residual(trim(s1, (0, 2)), (10, 0)))
    rhs = jnp.pad(rhs, ((1, 1), (0, 0), (0, 0)))
    perm = coarsen(trim(k1, (1, 5)))
    size_y2 = rhs.shape[1]
    k2, b2 = lax.all_gather(jnp.stack([perm, rhs]), "col", axis=2, tiled=True)
    lev2 = Band(faces_of(wrap_y(k2), scales[2]), 5, b2, 6)
    p = lev2.first_sweep(5)
    s2 = lev2.sweep(p, 4)
    rhs = coarsen(lev2.residual(s2[3:-3]))
    perm = coarsen(trim(k2, 6))
    correction = coarse_solve(rhs, perm, scales[3])
    q = s2 + prolong(correction)
    q = lev2.sweep(q, 3)
    u2 = lev2.sweep(q, 2)
    col = lax.axis_index("col")
    u2 = lax.dynamic_slice_in_dim(wrap_y(u2, 2), col * size_y2, size_y2 + 4, axis=1)
    q = trim(s1, (8, 0)) + trim(prolong(u2), (1, 1))
    q = lev1.sweep(q, (2, 2))
    u1 = lev1.sweep(q, (1, 1))
    q = s0 + prolong(u1)
    q = lev0.sweep(q, (1, 1))
    return lev0.sweep(q, (0, 0))


def solution(mesh):
    placed = (P("row", "col", None), P("row", "col", None), P("row", "col", None))
    return jax.shard_map(
        on_device, mesh=mesh, in_specs=placed, out_specs=P("row", "col", None), check_vma=False
    )
```

```python
import jax
import jax.numpy as jnp
from jax import lax
from jax.experimental import pallas as pl
from jax.experimental.pallas import tpu as pltpu
from jax.sharding import PartitionSpec as P

LEVELS = 3
NU1 = 2
NU2 = 2
CSWEEPS = 16

OMEGA = 0.8


def shift_from(x, axis, k):
    n = lax.axis_size(axis)
    return lax.ppermute(x, axis, [(i, (i + k) % n) for i in range(n)])


def halo(x, w):
    size_y = x.shape[-2]
    lower = shift_from(x[..., :, size_y - w :, :], "col", 1)
    upper = shift_from(x[..., :, :w, :], "col", -1)
    x = jnp.concatenate([lower, x, upper], axis=-2)
    size_x = x.shape[-3]
    lower = shift_from(x[..., size_x - w :, :, :], "row", 1)
    upper = shift_from(x[..., :w, :, :], "row", -1)
    return jnp.concatenate([lower, x, upper], axis=-3)


def trim(a, t, y=True):
    if t == 0:
        return a
    if y:
        return a[t:-t, t:-t]
    return a[t:-t]


def harmonic(left, right, scale):
    return 2.0 * left * right / (left + right) * scale


def faces_of(k, scale):
    c = k[1:-1, 1:-1]
    west_x = harmonic(k[:-2, 1:-1], c, scale)
    east_x = harmonic(c, k[2:, 1:-1], scale)
    west_y = harmonic(k[1:-1, :-2], c, scale)
    east_y = harmonic(c, k[1:-1, 2:], scale)
    inner = harmonic(c[:, :, :-1], c[:, :, 1:], scale)
    below = jnp.concatenate([2.0 * c[:, :, :1] * scale, inner], axis=2)
    above = jnp.concatenate([inner, 2.0 * c[:, :, -1:] * scale], axis=2)
    diagonal = west_x + east_x + west_y + east_y + below + above
    return (west_x, east_x, west_y, east_y, below, above, diagonal)


def apply_operator(v, faces):
    west_x, east_x, west_y, east_y, below, above, diagonal = faces
    c = v[1:-1, 1:-1]
    zero_plane = jnp.zeros_like(c[:, :, :1])
    under = jnp.concatenate([zero_plane, c[:, :, :-1]], axis=2)
    over = jnp.concatenate([c[:, :, 1:], zero_plane], axis=2)
    beside_all = west_x * v[:-2, 1:-1] + east_x * v[2:, 1:-1]
    beside_all = beside_all + west_y * v[1:-1, :-2] + east_y * v[1:-1, 2:]
    beside_all = beside_all + below * under + above * over
    return diagonal * c - beside_all


class Level:
    def __init__(self, faces, have, right_side, rhs_have):
        self.faces, self.have = faces, have
        self.right_side, self.rhs_have = right_side, rhs_have

    def faces_at(self, h, y=True):
        return tuple(trim(f, self.have - h, y) for f in self.faces)

    def rhs_at(self, h, y=True):
        return trim(self.right_side, self.rhs_have - h, y)

    def sweep(self, v, h):
        faces = self.faces_at(h)
        residual = self.rhs_at(h) - apply_operator(v, faces)
        return v[1:-1, 1:-1] + OMEGA * residual / faces[6]

    def first_sweep(self, h):
        return OMEGA * self.rhs_at(h) / self.faces_at(h)[6]

    def residual(self, v):
        return self.rhs_at(0) - apply_operator(v, self.faces_at(0))


def pairs(n):
    i = lax.broadcasted_iota(jnp.int32, (n, n // 2), 0)
    j = lax.broadcasted_iota(jnp.int32, (n, n // 2), 1)
    return (i // 2 == j).astype(jnp.float32)


def along_z(field, matrix):
    size_x, size_y, size_z = field.shape
    flat = field.reshape(size_x * size_y, size_z)
    out = jnp.dot(flat, matrix, precision=lax.Precision.HIGHEST)
    return out.reshape(size_x, size_y, matrix.shape[1])


def along_y(field, matrix):
    size_x = field.shape[0]
    batched = jnp.broadcast_to(matrix, (size_x,) + matrix.shape)
    return jnp.einsum("xjy,xyz->xjz", batched, field, precision=lax.Precision.HIGHEST)


def coarsen(field):
    size_x, size_y, size_z = field.shape
    t = field.reshape(size_x // 2, 2, size_y, size_z)
    t = t[:, 0] + t[:, 1]
    t = along_z(t, pairs(size_z))
    t = along_y(t, pairs(size_y).T)
    return t * 0.125


def prolong(field):
    size_x, size_y, size_z = field.shape
    t = along_z(field, pairs(2 * size_z).T)
    t = along_y(t, pairs(2 * size_y))
    t = jnp.broadcast_to(t[:, None], (size_x, 2) + t.shape[1:])
    return t.reshape(2 * size_x, 2 * size_y, 2 * size_z)


def wrap_y(a, w=1):
    return jnp.concatenate([a[:, -w:], a, a[:, :w]], axis=1)


class Band(Level):
    def faces_at(self, h, y=False):
        return super().faces_at(h, False)

    def rhs_at(self, h, y=False):
        return super().rhs_at(h, False)

    def sweep(self, v, h):
        faces = self.faces_at(h)
        residual = self.rhs_at(h) - apply_operator(wrap_y(v), faces)
        return v[1:-1] + OMEGA * residual / faces[6]

    def residual(self, v):
        return self.rhs_at(0) - apply_operator(wrap_y(v), self.faces_at(0))


def x_halo(x, w):
    size_x = x.shape[-3]
    lower = shift_from(x[..., size_x - w :, :, :], "row", 1)
    upper = shift_from(x[..., :w, :, :], "row", -1)
    return jnp.concatenate([lower, x, upper], axis=-3)


def rows_around(x, steps, axis):
    lower = [shift_from(x, "row", k) for k in reversed(steps)]
    upper = [shift_from(x, "row", -k) for k in steps]
    return jnp.concatenate(lower + [x] + upper, axis=axis)


def coarse_kernel(scale, size_z, spans, keep, lower_ref, own_ref, upper_ref, out_ref, tile_ref):
    span, extra = spans
    for f in range(2):
        tile_ref[f, 0:extra] = lower_ref[f]
        tile_ref[f, extra : extra + span] = own_ref[f]
        tile_ref[f, extra + span : 2 * extra + span] = upper_ref[f]
    b = tile_ref[0]
    k = tile_ref[1]
    rows, lanes = k.shape
    lane = lax.broadcasted_iota(jnp.int32, (rows, lanes), 1) % size_z
    first, last = lane == 0, lane == size_z - 1

    def x_lower(a):
        return pltpu.roll(a, 1, 0)

    def x_upper(a):
        return pltpu.roll(a, rows - 1, 0)

    def y_lower(a):
        return pltpu.roll(a, size_z, 1)

    def y_upper(a):
        return pltpu.roll(a, lanes - size_z, 1)

    def z_lower(a):
        return pltpu.roll(a, 1, 1)

    def z_upper(a):
        return pltpu.roll(a, lanes - 1, 1)

    west_x = harmonic(x_lower(k), k, scale)
    east_x = harmonic(k, x_upper(k), scale)
    west_y = harmonic(y_lower(k), k, scale)
    east_y = harmonic(k, y_upper(k), scale)
    below = jnp.where(first, 2.0 * k * scale, harmonic(z_lower(k), k, scale))
    above = jnp.where(last, 2.0 * k * scale, harmonic(k, z_upper(k), scale))
    diagonal = west_x + east_x + west_y + east_y + below + above

    def one_sweep(i, v):
        under = jnp.where(first, 0.0, z_lower(v))
        over = jnp.where(last, 0.0, z_upper(v))
        beside_all = west_x * x_lower(v) + east_x * x_upper(v)
        beside_all = beside_all + west_y * y_lower(v) + east_y * y_upper(v)
        beside_all = beside_all + below * under + above * over
        return v + OMEGA * (b - (diagonal * v - beside_all)) / diagonal

    v = OMEGA * b / diagonal
    v = lax.fori_loop(1, CSWEEPS, one_sweep, v)
    out_ref[...] = v[(rows - keep) // 2 : (rows + keep) // 2]


def coarse_solve(right_side, perm, scale):
    size_x, size_y, size_z = right_side.shape
    lanes = size_y * size_z
    pair = jnp.stack([right_side, perm]).reshape(2, size_x, lanes)
    near = rows_around(pair, (1, 2), 1)
    span = near.shape[1]
    extra = CSWEEPS + 2 - (span - size_x) // 2
    extra += (-(span + 2 * extra)) % 8 // 2
    assert 0 < extra <= span
    rows = span + 2 * extra
    keep = 8
    assert (rows - keep) // 2 >= CSWEEPS
    lower = shift_from(near[:, span - extra :], "row", 5)
    upper = shift_from(near[:, :extra], "row", -5)
    call = pl.pallas_call(
        lambda *refs: coarse_kernel(scale, size_z, (span, extra), keep, *refs),
        out_shape=jax.ShapeDtypeStruct((keep, lanes), jnp.float32),
        scratch_shapes=[pltpu.VMEM((2, rows, lanes), jnp.float32)],
        cost_estimate=pl.CostEstimate(
            flops=40 * CSWEEPS * rows * lanes, transcendentals=0, bytes_accessed=24 * rows * lanes
        ),
    )
    v = call(lower, near, upper)
    return v.reshape(keep, size_y, size_z)


def on_device(pressure_in, source, permeability):
    scales = [0.25**level for level in range(LEVELS + 1)]
    k0, p0, b0 = halo(jnp.stack([permeability, pressure_in, source]), 4)
    lev0 = Level(faces_of(k0, scales[0]), 3, b0, 4)
    p = lev0.sweep(p0, 3)
    s0 = lev0.sweep(p, 2)
    rhs = coarsen(lev0.residual(trim(s0, 1)))
    perm = coarsen(permeability)
    k1, b1 = halo(jnp.stack([perm, rhs]), 5)
    lev1 = Level(faces_of(k1, scales[1]), 4, b1, 5)
    p = lev1.first_sweep(4)
    s1 = lev1.sweep(p, 3)
    rhs = coarsen(lev1.residual(trim(s1, 2)))
    perm = coarsen(perm)
    size_y2 = rhs.shape[1]
    band = lax.all_gather(jnp.stack([perm, rhs]), "col", axis=2, tiled=True)
    k2, b2 = x_halo(band, 4)
    lev2 = Band(faces_of(wrap_y(k2), scales[2]), 3, b2, 4)
    p = lev2.first_sweep(3)
    s2 = lev2.sweep(p, 2)
    rhs = coarsen(lev2.residual(s2[1:-1]))
    perm = coarsen(band[0])
    correction = coarse_solve(rhs, perm, scales[3])
    q = s2 + prolong(correction)[2:-2]
    q = lev2.sweep(q, 1)
    u2 = lev2.sweep(q, 0)
    u2 = wrap_y(x_halo(u2, 2), 2)
    col = lax.axis_index("col")
    u2 = lax.dynamic_slice_in_dim(u2, col * size_y2, size_y2 + 4, axis=1)
    q = s1 + trim(prolong(u2), 1)
    q = lev1.sweep(q, 2)
    u1 = lev1.sweep(q, 1)
    q = s0 + prolong(u1)
    q = lev0.sweep(q, 1)
    return lev0.sweep(q, 0)


def solution(mesh):
    placed = (P("row", "col", None), P("row", "col", None), P("row", "col", None))
    return jax.shard_map(
        on_device, mesh=mesh, in_specs=placed, out_specs=P("row", "col", None), check_vma=False
    )
```

```python
import jax
import jax.numpy as jnp
from jax import lax
from jax.experimental import pallas as pl
from jax.experimental.pallas import tpu as pltpu
from jax.sharding import PartitionSpec as P

LEVELS = 3
NU1 = 2
NU2 = 2
CSWEEPS = 16

OMEGA = 0.8


def shift_from(x, axis, k):
    n = lax.axis_size(axis)
    return lax.ppermute(x, axis, [(i, (i + k) % n) for i in range(n)])


def halo(x, w):
    size_y = x.shape[-2]
    lower = shift_from(x[..., :, size_y - w :, :], "col", 1)
    upper = shift_from(x[..., :, :w, :], "col", -1)
    x = jnp.concatenate([lower, x, upper], axis=-2)
    size_x = x.shape[-3]
    lower = shift_from(x[..., size_x - w :, :, :], "row", 1)
    upper = shift_from(x[..., :w, :, :], "row", -1)
    return jnp.concatenate([lower, x, upper], axis=-3)


def trim(a, t, y=True):
    if t == 0:
        return a
    if y:
        return a[t:-t, t:-t]
    return a[t:-t]


def harmonic(left, right, scale):
    return 2.0 * left * right / (left + right) * scale


def faces_of(k, scale):
    c = k[1:-1, 1:-1]
    west_x = harmonic(k[:-2, 1:-1], c, scale)
    east_x = harmonic(c, k[2:, 1:-1], scale)
    west_y = harmonic(k[1:-1, :-2], c, scale)
    east_y = harmonic(c, k[1:-1, 2:], scale)
    inner = harmonic(c[:, :, :-1], c[:, :, 1:], scale)
    below = jnp.concatenate([2.0 * c[:, :, :1] * scale, inner], axis=2)
    above = jnp.concatenate([inner, 2.0 * c[:, :, -1:] * scale], axis=2)
    diagonal = west_x + east_x + west_y + east_y + below + above
    return (west_x, east_x, west_y, east_y, below, above, diagonal)


def apply_operator(v, faces):
    west_x, east_x, west_y, east_y, below, above, diagonal = faces
    c = v[1:-1, 1:-1]
    zero_plane = jnp.zeros_like(c[:, :, :1])
    under = jnp.concatenate([zero_plane, c[:, :, :-1]], axis=2)
    over = jnp.concatenate([c[:, :, 1:], zero_plane], axis=2)
    beside_all = west_x * v[:-2, 1:-1] + east_x * v[2:, 1:-1]
    beside_all = beside_all + west_y * v[1:-1, :-2] + east_y * v[1:-1, 2:]
    beside_all = beside_all + below * under + above * over
    return diagonal * c - beside_all


class Level:
    def __init__(self, faces, have, right_side, rhs_have):
        self.faces, self.have = faces, have
        self.right_side, self.rhs_have = right_side, rhs_have

    def faces_at(self, h, y=True):
        return tuple(trim(f, self.have - h, y) for f in self.faces)

    def rhs_at(self, h, y=True):
        return trim(self.right_side, self.rhs_have - h, y)

    def sweep(self, v, h):
        faces = self.faces_at(h)
        residual = self.rhs_at(h) - apply_operator(v, faces)
        return v[1:-1, 1:-1] + OMEGA * residual / faces[6]

    def first_sweep(self, h):
        return OMEGA * self.rhs_at(h) / self.faces_at(h)[6]

    def residual(self, v):
        return self.rhs_at(0) - apply_operator(v, self.faces_at(0))


def pairs(n):
    i = lax.broadcasted_iota(jnp.int32, (n, n // 2), 0)
    j = lax.broadcasted_iota(jnp.int32, (n, n // 2), 1)
    return (i // 2 == j).astype(jnp.float32)


def along_z(field, matrix):
    size_x, size_y, size_z = field.shape
    flat = field.reshape(size_x * size_y, size_z)
    out = jnp.dot(flat, matrix, precision=lax.Precision.HIGHEST)
    return out.reshape(size_x, size_y, matrix.shape[1])


def along_y(field, matrix):
    size_x = field.shape[0]
    batched = jnp.broadcast_to(matrix, (size_x,) + matrix.shape)
    return jnp.einsum("xjy,xyz->xjz", batched, field, precision=lax.Precision.HIGHEST)


def coarsen(field):
    size_x, size_y, size_z = field.shape
    t = field.reshape(size_x // 2, 2, size_y, size_z)
    t = t[:, 0] + t[:, 1]
    t = along_z(t, pairs(size_z))
    t = along_y(t, pairs(size_y).T)
    return t * 0.125


def prolong(field):
    size_x, size_y, size_z = field.shape
    t = along_z(field, pairs(2 * size_z).T)
    t = along_y(t, pairs(2 * size_y))
    t = jnp.broadcast_to(t[:, None], (size_x, 2) + t.shape[1:])
    return t.reshape(2 * size_x, 2 * size_y, 2 * size_z)


def wrap_y(a, w=1):
    return jnp.concatenate([a[:, -w:], a, a[:, :w]], axis=1)


def faces_band(k, scale):
    c = k[1:-1]
    west_x = harmonic(k[:-2], c, scale)
    east_x = harmonic(c, k[2:], scale)
    west_y = harmonic(jnp.roll(c, 1, axis=2), c, scale)
    east_y = harmonic(c, jnp.roll(c, -1, axis=2), scale)
    inner = harmonic(c[:, :-1], c[:, 1:], scale)
    below = jnp.concatenate([2.0 * c[:, :1] * scale, inner], axis=1)
    above = jnp.concatenate([inner, 2.0 * c[:, -1:] * scale], axis=1)
    diagonal = west_x + east_x + west_y + east_y + below + above
    return (west_x, east_x, west_y, east_y, below, above, diagonal)


def apply_band(v, faces):
    west_x, east_x, west_y, east_y, below, above, diagonal = faces
    c = v[1:-1]
    zero_plane = jnp.zeros_like(c[:, :1])
    under = jnp.concatenate([zero_plane, c[:, :-1]], axis=1)
    over = jnp.concatenate([c[:, 1:], zero_plane], axis=1)
    beside_all = west_x * v[:-2] + east_x * v[2:]
    beside_all = beside_all + west_y * jnp.roll(c, 1, axis=2) + east_y * jnp.roll(c, -1, axis=2)
    beside_all = beside_all + below * under + above * over
    return diagonal * c - beside_all


class Band(Level):
    def faces_at(self, h, y=False):
        return super().faces_at(h, False)

    def rhs_at(self, h, y=False):
        return super().rhs_at(h, False)

    def sweep(self, v, h):
        faces = self.faces_at(h)
        residual = self.rhs_at(h) - apply_band(v, faces)
        return v[1:-1] + OMEGA * residual / faces[6]

    def residual(self, v):
        return self.rhs_at(0) - apply_band(v, self.faces_at(0))


def x_halo(x, w):
    size_x = x.shape[-3]
    lower = shift_from(x[..., size_x - w :, :, :], "row", 1)
    upper = shift_from(x[..., :w, :, :], "row", -1)
    return jnp.concatenate([lower, x, upper], axis=-3)


def rows_around(x, steps, axis):
    lower = [shift_from(x, "row", k) for k in reversed(steps)]
    upper = [shift_from(x, "row", -k) for k in steps]
    return jnp.concatenate(lower + [x] + upper, axis=axis)


def coarse_kernel(scale, size_y, spans, keep, lower_ref, own_ref, upper_ref, out_ref, tile_ref):
    span, extra = spans
    for f in range(2):
        tile_ref[f, 0:extra] = lower_ref[f]
        tile_ref[f, extra : extra + span] = own_ref[f]
        tile_ref[f, extra + span : 2 * extra + span] = upper_ref[f]
    b = tile_ref[0]
    k = tile_ref[1]
    rows, lanes = k.shape
    lane = lax.broadcasted_iota(jnp.int32, (rows, lanes), 1)
    first, last = lane < size_y, lane >= lanes - size_y
    y_first, y_last = lane % size_y == 0, lane % size_y == size_y - 1

    def x_lower(a):
        return pltpu.roll(a, 1, 0)

    def x_upper(a):
        return pltpu.roll(a, rows - 1, 0)

    def y_lower(a):
        return jnp.where(y_first, pltpu.roll(a, lanes - (size_y - 1), 1), pltpu.roll(a, 1, 1))

    def y_upper(a):
        return jnp.where(y_last, pltpu.roll(a, size_y - 1, 1), pltpu.roll(a, lanes - 1, 1))

    def z_lower(a):
        return pltpu.roll(a, size_y, 1)

    def z_upper(a):
        return pltpu.roll(a, lanes - size_y, 1)

    west_x = harmonic(x_lower(k), k, scale)
    east_x = harmonic(k, x_upper(k), scale)
    west_y = harmonic(y_lower(k), k, scale)
    east_y = harmonic(k, y_upper(k), scale)
    below = jnp.where(first, 2.0 * k * scale, harmonic(z_lower(k), k, scale))
    above = jnp.where(last, 2.0 * k * scale, harmonic(k, z_upper(k), scale))
    diagonal = west_x + east_x + west_y + east_y + below + above

    def one_sweep(i, v):
        under = jnp.where(first, 0.0, z_lower(v))
        over = jnp.where(last, 0.0, z_upper(v))
        beside_all = west_x * x_lower(v) + east_x * x_upper(v)
        beside_all = beside_all + west_y * y_lower(v) + east_y * y_upper(v)
        beside_all = beside_all + below * under + above * over
        return v + OMEGA * (b - (diagonal * v - beside_all)) / diagonal

    v = OMEGA * b / diagonal
    v = lax.fori_loop(1, CSWEEPS, one_sweep, v)
    out_ref[...] = v[(rows - keep) // 2 : (rows + keep) // 2]


def coarse_solve(right_side, perm, scale):
    size_x, size_z, size_y = right_side.shape
    lanes = size_y * size_z
    pair = jnp.stack([right_side, perm]).reshape(2, size_x, lanes)
    near = rows_around(pair, (1, 2), 1)
    span = near.shape[1]
    extra = CSWEEPS + 2 - (span - size_x) // 2
    extra += (-(span + 2 * extra)) % 8 // 2
    assert 0 < extra <= span
    rows = span + 2 * extra
    keep = 8
    assert (rows - keep) // 2 >= CSWEEPS
    lower = shift_from(near[:, span - extra :], "row", 5)
    upper = shift_from(near[:, :extra], "row", -5)
    call = pl.pallas_call(
        lambda *refs: coarse_kernel(scale, size_y, (span, extra), keep, *refs),
        out_shape=jax.ShapeDtypeStruct((keep, lanes), jnp.float32),
        scratch_shapes=[pltpu.VMEM((2, rows, lanes), jnp.float32)],
        cost_estimate=pl.CostEstimate(
            flops=40 * CSWEEPS * rows * lanes, transcendentals=0, bytes_accessed=24 * rows * lanes
        ),
    )
    v = call(lower, near, upper)
    return v.reshape(keep, size_z, size_y)


def on_device(pressure_in, source, permeability):
    scales = [0.25**level for level in range(LEVELS + 1)]
    k0, p0, b0 = halo(jnp.stack([permeability, pressure_in, source]), 4)
    lev0 = Level(faces_of(k0, scales[0]), 3, b0, 4)
    p = lev0.sweep(p0, 3)
    s0 = lev0.sweep(p, 2)
    rhs = coarsen(lev0.residual(trim(s0, 1)))
    perm = coarsen(permeability)
    k1, b1 = halo(jnp.stack([perm, rhs]), 5)
    lev1 = Level(faces_of(k1, scales[1]), 4, b1, 5)
    p = lev1.first_sweep(4)
    s1 = lev1.sweep(p, 3)
    rhs = coarsen(lev1.residual(trim(s1, 2)))
    perm = coarsen(perm)
    size_y2 = rhs.shape[1]
    block = jnp.swapaxes(jnp.stack([perm, rhs]), 2, 3)
    band = lax.all_gather(block, "col", axis=3, tiled=True)
    k2, b2 = x_halo(band, 4)
    lev2 = Band(faces_band(k2, scales[2]), 3, b2, 4)
    p = lev2.first_sweep(3)
    s2 = lev2.sweep(p, 2)
    rhs = coarsen(lev2.residual(s2[1:-1]))
    perm = coarsen(band[0])
    correction = coarse_solve(rhs, perm, scales[3])
    q = s2 + prolong(correction)[2:-2]
    q = lev2.sweep(q, 1)
    u2 = lev2.sweep(q, 0)
    u2 = x_halo(u2, 2)
    u2 = jnp.concatenate([u2[..., -2:], u2, u2[..., :2]], axis=2)
    col = lax.axis_index("col")
    u2 = lax.dynamic_slice_in_dim(u2, col * size_y2, size_y2 + 4, axis=2)
    u2 = jnp.swapaxes(u2, 1, 2)
    q = s1 + trim(prolong(u2), 1)
    q = lev1.sweep(q, 2)
    u1 = lev1.sweep(q, 1)
    q = s0 + prolong(u1)
    q = lev0.sweep(q, 1)
    return lev0.sweep(q, 0)


def solution(mesh):
    placed = (P("row", "col", None), P("row", "col", None), P("row", "col", None))
    return jax.shard_map(
        on_device, mesh=mesh, in_specs=placed, out_specs=P("row", "col", None), check_vma=False
    )
```

```python
import jax
import jax.numpy as jnp
from jax import lax
from jax.experimental import pallas as pl
from jax.experimental.pallas import tpu as pltpu
from jax.sharding import PartitionSpec as P

LEVELS = 3
NU1 = 2
NU2 = 2
CSWEEPS = 16

OMEGA = 0.8


def shift_from(x, axis, k):
    n = lax.axis_size(axis)
    return lax.ppermute(x, axis, [(i, (i + k) % n) for i in range(n)])


def halo(x, w):
    size_y = x.shape[-2]
    lower = shift_from(x[..., :, size_y - w :, :], "col", 1)
    upper = shift_from(x[..., :, :w, :], "col", -1)
    x = jnp.concatenate([lower, x, upper], axis=-2)
    size_x = x.shape[-3]
    lower = shift_from(x[..., size_x - w :, :, :], "row", 1)
    upper = shift_from(x[..., :w, :, :], "row", -1)
    return jnp.concatenate([lower, x, upper], axis=-3)


def trim(a, t, y=True):
    if t == 0:
        return a
    if y:
        return a[t:-t, t:-t]
    return a[t:-t]


def harmonic(left, right, scale):
    return 2.0 * left * right / (left + right) * scale


def faces_of(k, scale):
    c = k[1:-1, 1:-1]
    west_x = harmonic(k[:-2, 1:-1], c, scale)
    east_x = harmonic(c, k[2:, 1:-1], scale)
    west_y = harmonic(k[1:-1, :-2], c, scale)
    east_y = harmonic(c, k[1:-1, 2:], scale)
    inner = harmonic(c[:, :, :-1], c[:, :, 1:], scale)
    below = jnp.concatenate([2.0 * c[:, :, :1] * scale, inner], axis=2)
    above = jnp.concatenate([inner, 2.0 * c[:, :, -1:] * scale], axis=2)
    diagonal = west_x + east_x + west_y + east_y + below + above
    return (west_x, east_x, west_y, east_y, below, above, diagonal)


def apply_operator(v, faces):
    west_x, east_x, west_y, east_y, below, above, diagonal = faces
    c = v[1:-1, 1:-1]
    zero_plane = jnp.zeros_like(c[:, :, :1])
    under = jnp.concatenate([zero_plane, c[:, :, :-1]], axis=2)
    over = jnp.concatenate([c[:, :, 1:], zero_plane], axis=2)
    beside_all = west_x * v[:-2, 1:-1] + east_x * v[2:, 1:-1]
    beside_all = beside_all + west_y * v[1:-1, :-2] + east_y * v[1:-1, 2:]
    beside_all = beside_all + below * under + above * over
    return diagonal * c - beside_all


class Level:
    def __init__(self, faces, have, right_side, rhs_have):
        self.faces, self.have = faces, have
        self.right_side, self.rhs_have = right_side, rhs_have

    def faces_at(self, h, y=True):
        return tuple(trim(f, self.have - h, y) for f in self.faces)

    def rhs_at(self, h, y=True):
        return trim(self.right_side, self.rhs_have - h, y)

    def sweep(self, v, h):
        faces = self.faces_at(h)
        residual = self.rhs_at(h) - apply_operator(v, faces)
        return v[1:-1, 1:-1] + OMEGA * residual / faces[6]

    def first_sweep(self, h):
        return OMEGA * self.rhs_at(h) / self.faces_at(h)[6]

    def residual(self, v):
        return self.rhs_at(0) - apply_operator(v, self.faces_at(0))


def pairs(n):
    i = lax.broadcasted_iota(jnp.int32, (n, n // 2), 0)
    j = lax.broadcasted_iota(jnp.int32, (n, n // 2), 1)
    return (i // 2 == j).astype(jnp.float32)


def along_z(field, matrix):
    size_x, size_y, size_z = field.shape
    flat = field.reshape(size_x * size_y, size_z)
    out = jnp.dot(flat, matrix, precision=lax.Precision.HIGHEST)
    return out.reshape(size_x, size_y, matrix.shape[1])


def along_y(field, matrix):
    size_x = field.shape[0]
    batched = jnp.broadcast_to(matrix, (size_x,) + matrix.shape)
    return jnp.einsum("xjy,xyz->xjz", batched, field, precision=lax.Precision.HIGHEST)


def coarsen(field):
    size_x, size_y, size_z = field.shape
    t = field.reshape(size_x // 2, 2, size_y, size_z)
    t = t[:, 0] + t[:, 1]
    t = along_z(t, pairs(size_z))
    t = along_y(t, pairs(size_y).T)
    return t * 0.125


def prolong(field):
    size_x, size_y, size_z = field.shape
    t = along_z(field, pairs(2 * size_z).T)
    t = along_y(t, pairs(2 * size_y))
    t = jnp.broadcast_to(t[:, None], (size_x, 2) + t.shape[1:])
    return t.reshape(2 * size_x, 2 * size_y, 2 * size_z)


def wrap_y(a, w=1):
    return jnp.concatenate([a[:, -w:], a, a[:, :w]], axis=1)


def lane_band_ops(size_z):
    def roll(a, k, axis):
        return jnp.roll(a, k, axis=axis)

    def masks(a):
        lane = lax.broadcasted_iota(jnp.int32, a.shape, 2)
        size_l = a.shape[2]
        return lane % size_z == 0, lane % size_z == size_z - 1, lane < size_z, lane >= size_l - size_z

    def y_lower(a):
        _, _, y_first, _ = masks(a)
        inside = roll(a, size_z, 2)
        return jnp.where(y_first, roll(inside, 1, 0), inside)

    def y_upper(a):
        _, _, _, y_last = masks(a)
        inside = roll(a, -size_z, 2)
        return jnp.where(y_last, roll(inside, -1, 0), inside)

    def faces(k, scale):
        first, last, _, _ = masks(k[:, 1:-1])
        c = k[:, 1:-1]
        west_x = harmonic(k[:, :-2], c, scale)
        east_x = harmonic(c, k[:, 2:], scale)
        west_y = harmonic(y_lower(c), c, scale)
        east_y = harmonic(c, y_upper(c), scale)
        below = jnp.where(first, 2.0 * c * scale, harmonic(roll(c, 1, 2), c, scale))
        above = jnp.where(last, 2.0 * c * scale, harmonic(c, roll(c, -1, 2), scale))
        diagonal = west_x + east_x + west_y + east_y + below + above
        return (west_x, east_x, west_y, east_y, below, above, diagonal)

    def apply(v, faces):
        west_x, east_x, west_y, east_y, below, above, diagonal = faces
        c = v[:, 1:-1]
        first, last, _, _ = masks(c)
        under = jnp.where(first, 0.0, roll(c, 1, 2))
        over = jnp.where(last, 0.0, roll(c, -1, 2))
        beside_all = west_x * v[:, :-2] + east_x * v[:, 2:]
        beside_all = beside_all + west_y * y_lower(c) + east_y * y_upper(c)
        beside_all = beside_all + below * under + above * over
        return diagonal * c - beside_all

    return faces, apply


class LaneBand:
    def __init__(self, ops, k, scale, have, right_side, rhs_have):
        faces, self.apply = ops
        self.faces, self.have = faces(k, scale), have
        self.right_side, self.rhs_have = right_side, rhs_have

    def faces_at(self, h):
        t = self.have - h
        return tuple(f[:, t : f.shape[1] - t] for f in self.faces)

    def rhs_at(self, h):
        t = self.rhs_have - h
        return self.right_side[:, t : self.right_side.shape[1] - t]

    def sweep(self, v, h):
        faces = self.faces_at(h)
        residual = self.rhs_at(h) - self.apply(v, faces)
        return v[:, 1:-1] + OMEGA * residual / faces[6]

    def first_sweep(self, h):
        return OMEGA * self.rhs_at(h) / self.faces_at(h)[6]

    def residual(self, v):
        return self.rhs_at(0) - self.apply(v, self.faces_at(0))


def lane_pairs(size_y, size_z):
    n = size_y * size_z
    i = lax.broadcasted_iota(jnp.int32, (n, n // 4), 0)
    j = lax.broadcasted_iota(jnp.int32, (n, n // 4), 1)
    coarse = (i // size_z // 2) * (size_z // 2) + (i % size_z) // 2
    return (coarse == j).astype(jnp.float32)


def band_coarsen(field, size_y, size_z):
    t = along_y(field, pairs(field.shape[1]).T)
    t = jnp.einsum("cxl,lm->cxm", t, lane_pairs(size_y, size_z), precision=lax.Precision.HIGHEST)
    return t * 0.125


def band_prolong(field, size_y, size_z):
    t = jnp.einsum("cxm,lm->cxl", field, lane_pairs(size_y, size_z), precision=lax.Precision.HIGHEST)
    return along_y(t, pairs(2 * field.shape[1]))


def rows_halo(x, w, axis):
    size_x = x.shape[axis]
    lower = shift_from(lax.slice_in_dim(x, size_x - w, size_x, axis=axis), "row", 1)
    upper = shift_from(lax.slice_in_dim(x, 0, w, axis=axis), "row", -1)
    return jnp.concatenate([lower, x, upper], axis=axis)


def x_halo(x, w):
    size_x = x.shape[-3]
    lower = shift_from(x[..., size_x - w :, :, :], "row", 1)
    upper = shift_from(x[..., :w, :, :], "row", -1)
    return jnp.concatenate([lower, x, upper], axis=-3)


def rows_around(x, steps, axis):
    lower = [shift_from(x, "row", k) for k in reversed(steps)]
    upper = [shift_from(x, "row", -k) for k in steps]
    return jnp.concatenate(lower + [x] + upper, axis=axis)


def coarse_kernel(scale, size_z, spans, keep, lower_ref, own_ref, upper_ref, out_ref, tile_ref):
    span, extra = spans
    for f in range(2):
        tile_ref[f, 0:extra] = lower_ref[f]
        tile_ref[f, extra : extra + span] = own_ref[f]
        tile_ref[f, extra + span : 2 * extra + span] = upper_ref[f]
    b = tile_ref[0]
    k = tile_ref[1]
    rows, lanes = k.shape
    lane = lax.broadcasted_iota(jnp.int32, (rows, lanes), 1) % size_z
    first, last = lane == 0, lane == size_z - 1

    def x_lower(a):
        return pltpu.roll(a, 1, 0)

    def x_upper(a):
        return pltpu.roll(a, rows - 1, 0)

    def y_lower(a):
        return pltpu.roll(a, size_z, 1)

    def y_upper(a):
        return pltpu.roll(a, lanes - size_z, 1)

    def z_lower(a):
        return pltpu.roll(a, 1, 1)

    def z_upper(a):
        return pltpu.roll(a, lanes - 1, 1)

    west_x = harmonic(x_lower(k), k, scale)
    east_x = harmonic(k, x_upper(k), scale)
    west_y = harmonic(y_lower(k), k, scale)
    east_y = harmonic(k, y_upper(k), scale)
    below = jnp.where(first, 2.0 * k * scale, harmonic(z_lower(k), k, scale))
    above = jnp.where(last, 2.0 * k * scale, harmonic(k, z_upper(k), scale))
    diagonal = west_x + east_x + west_y + east_y + below + above

    def one_sweep(i, v):
        under = jnp.where(first, 0.0, z_lower(v))
        over = jnp.where(last, 0.0, z_upper(v))
        beside_all = west_x * x_lower(v) + east_x * x_upper(v)
        beside_all = beside_all + west_y * y_lower(v) + east_y * y_upper(v)
        beside_all = beside_all + below * under + above * over
        return v + OMEGA * (b - (diagonal * v - beside_all)) / diagonal

    v = OMEGA * b / diagonal
    v = lax.fori_loop(1, CSWEEPS, one_sweep, v)
    out_ref[...] = v[(rows - keep) // 2 : (rows + keep) // 2]


def coarse_solve(pair, size_z, scale):
    size_x, lanes = pair.shape[1:]
    near = rows_around(pair, (1, 2), 1)
    span = near.shape[1]
    extra = CSWEEPS + 2 - (span - size_x) // 2
    extra += (-(span + 2 * extra)) % 8 // 2
    assert 0 < extra <= span
    rows = span + 2 * extra
    keep = 8
    assert (rows - keep) // 2 >= CSWEEPS
    lower = shift_from(near[:, span - extra :], "row", 5)
    upper = shift_from(near[:, :extra], "row", -5)
    call = pl.pallas_call(
        lambda *refs: coarse_kernel(scale, size_z, (span, extra), keep, *refs),
        out_shape=jax.ShapeDtypeStruct((keep, lanes), jnp.float32),
        scratch_shapes=[pltpu.VMEM((2, rows, lanes), jnp.float32)],
        cost_estimate=pl.CostEstimate(
            flops=40 * CSWEEPS * rows * lanes, transcendentals=0, bytes_accessed=24 * rows * lanes
        ),
    )
    return call(lower, near, upper)


def on_device(pressure_in, source, permeability):
    scales = [0.25**level for level in range(LEVELS + 1)]
    k0, p0, b0 = halo(jnp.stack([permeability, pressure_in, source]), 4)
    lev0 = Level(faces_of(k0, scales[0]), 3, b0, 4)
    p = lev0.sweep(p0, 3)
    s0 = lev0.sweep(p, 2)
    rhs = coarsen(lev0.residual(trim(s0, 1)))
    perm = coarsen(permeability)
    k1, b1 = halo(jnp.stack([perm, rhs]), 5)
    lev1 = Level(faces_of(k1, scales[1]), 4, b1, 5)
    p = lev1.first_sweep(4)
    s1 = lev1.sweep(p, 3)
    rhs = coarsen(lev1.residual(trim(s1, 2)))
    perm = coarsen(perm)
    _, size_y2, size_z2 = rhs.shape
    block = jnp.stack([perm, rhs]).reshape(2, rhs.shape[0], size_y2 * size_z2)
    band = lax.all_gather(block, "col", axis=0, tiled=False)
    k2, b2 = jnp.moveaxis(rows_halo(band, 4, 2), 1, 0)
    ops = lane_band_ops(size_z2)
    lev2 = LaneBand(ops, k2, scales[2], 3, b2, 4)
    p = lev2.first_sweep(3)
    s2 = lev2.sweep(p, 2)
    rhs = band_coarsen(lev2.residual(s2[:, 1:-1]), size_y2, size_z2)
    perm = band_coarsen(band[:, 0], size_y2, size_z2)
    blocks, size_x3, lanes3 = rhs.shape
    pair = jnp.stack([rhs, perm], axis=1)
    pair = jnp.transpose(pair, (1, 2, 0, 3)).reshape(2, size_x3, blocks * lanes3)
    correction = coarse_solve(pair, size_z2 // 2, scales[3])
    correction = jnp.transpose(correction.reshape(-1, blocks, lanes3), (1, 0, 2))
    q = s2 + band_prolong(correction, size_y2, size_z2)[:, 2:-2]
    q = lev2.sweep(q, 1)
    u2 = lev2.sweep(q, 0)
    u2 = rows_halo(u2, 2, 1)
    u2 = jnp.concatenate([u2[-1:], u2, u2[:1]], axis=0)
    col = lax.axis_index("col")
    u2 = lax.dynamic_slice_in_dim(u2, col, 3, axis=0)
    edge = 2 * size_z2
    u2 = jnp.concatenate([u2[0, :, -edge:], u2[1], u2[2, :, :edge]], axis=1)
    u2 = u2.reshape(u2.shape[0], size_y2 + 4, size_z2)
    q = s1 + trim(prolong(u2), 1)
    q = lev1.sweep(q, 2)
    u1 = lev1.sweep(q, 1)
    q = s0 + prolong(u1)
    q = lev0.sweep(q, 1)
    return lev0.sweep(q, 0)


def solution(mesh):
    placed = (P("row", "col", None), P("row", "col", None), P("row", "col", None))
    return jax.shard_map(
        on_device, mesh=mesh, in_specs=placed, out_specs=P("row", "col", None), check_vma=False
    )
```

```python
import jax
import jax.numpy as jnp
from jax import lax
from jax.experimental import pallas as pl
from jax.experimental.pallas import tpu as pltpu
from jax.sharding import PartitionSpec as P

LEVELS = 3
NU1 = 2
NU2 = 2
CSWEEPS = 16

OMEGA = 0.8


def shift_from(x, axis, k):
    n = lax.axis_size(axis)
    return lax.ppermute(x, axis, [(i, (i + k) % n) for i in range(n)])


def halo(x, w):
    size_y = x.shape[-2]
    lower = shift_from(x[..., :, size_y - w :, :], "col", 1)
    upper = shift_from(x[..., :, :w, :], "col", -1)
    x = jnp.concatenate([lower, x, upper], axis=-2)
    size_x = x.shape[-3]
    lower = shift_from(x[..., size_x - w :, :, :], "row", 1)
    upper = shift_from(x[..., :w, :, :], "row", -1)
    return jnp.concatenate([lower, x, upper], axis=-3)


def trim(a, t, y=True):
    if t == 0:
        return a
    if y:
        return a[t:-t, t:-t]
    return a[t:-t]


def harmonic(left, right, scale):
    return 2.0 * left * right / (left + right) * scale


def faces_of(k, scale):
    c = k[1:-1, 1:-1]
    west_x = harmonic(k[:-2, 1:-1], c, scale)
    east_x = harmonic(c, k[2:, 1:-1], scale)
    west_y = harmonic(k[1:-1, :-2], c, scale)
    east_y = harmonic(c, k[1:-1, 2:], scale)
    inner = harmonic(c[:, :, :-1], c[:, :, 1:], scale)
    below = jnp.concatenate([2.0 * c[:, :, :1] * scale, inner], axis=2)
    above = jnp.concatenate([inner, 2.0 * c[:, :, -1:] * scale], axis=2)
    diagonal = west_x + east_x + west_y + east_y + below + above
    return (west_x, east_x, west_y, east_y, below, above, diagonal)


def apply_operator(v, faces):
    west_x, east_x, west_y, east_y, below, above, diagonal = faces
    c = v[1:-1, 1:-1]
    zero_plane = jnp.zeros_like(c[:, :, :1])
    under = jnp.concatenate([zero_plane, c[:, :, :-1]], axis=2)
    over = jnp.concatenate([c[:, :, 1:], zero_plane], axis=2)
    beside_all = west_x * v[:-2, 1:-1] + east_x * v[2:, 1:-1]
    beside_all = beside_all + west_y * v[1:-1, :-2] + east_y * v[1:-1, 2:]
    beside_all = beside_all + below * under + above * over
    return diagonal * c - beside_all


class Level:
    def __init__(self, faces, have, right_side, rhs_have):
        self.faces, self.have = faces, have
        self.right_side, self.rhs_have = right_side, rhs_have

    def faces_at(self, h, y=True):
        return tuple(trim(f, self.have - h, y) for f in self.faces)

    def rhs_at(self, h, y=True):
        return trim(self.right_side, self.rhs_have - h, y)

    def sweep(self, v, h):
        faces = self.faces_at(h)
        residual = self.rhs_at(h) - apply_operator(v, faces)
        return v[1:-1, 1:-1] + OMEGA * residual / faces[6]

    def first_sweep(self, h):
        return OMEGA * self.rhs_at(h) / self.faces_at(h)[6]

    def residual(self, v):
        return self.rhs_at(0) - apply_operator(v, self.faces_at(0))


def pairs(n):
    i = lax.broadcasted_iota(jnp.int32, (n, n // 2), 0)
    j = lax.broadcasted_iota(jnp.int32, (n, n // 2), 1)
    return (i // 2 == j).astype(jnp.float32)


def along_z(field, matrix):
    size_x, size_y, size_z = field.shape
    flat = field.reshape(size_x * size_y, size_z)
    out = jnp.dot(flat, matrix, precision=lax.Precision.HIGHEST)
    return out.reshape(size_x, size_y, matrix.shape[1])


def along_y(field, matrix):
    size_x = field.shape[0]
    batched = jnp.broadcast_to(matrix, (size_x,) + matrix.shape)
    return jnp.einsum("xjy,xyz->xjz", batched, field, precision=lax.Precision.HIGHEST)


def coarsen(field):
    size_x, size_y, size_z = field.shape
    t = field.reshape(size_x // 2, 2, size_y, size_z)
    t = t[:, 0] + t[:, 1]
    t = along_z(t, pairs(size_z))
    t = along_y(t, pairs(size_y).T)
    return t * 0.125


def prolong(field):
    size_x, size_y, size_z = field.shape
    t = along_z(field, pairs(2 * size_z).T)
    t = along_y(t, pairs(2 * size_y))
    t = jnp.broadcast_to(t[:, None], (size_x, 2) + t.shape[1:])
    return t.reshape(2 * size_x, 2 * size_y, 2 * size_z)


def wrap_y(a, w=1):
    return jnp.concatenate([a[:, -w:], a, a[:, :w]], axis=1)


def lane_band_ops(size_z):
    def roll(a, k, axis):
        return jnp.roll(a, k, axis=axis)

    def masks(a):
        lane = lax.broadcasted_iota(jnp.int32, a.shape, 2)
        size_l = a.shape[2]
        return lane % size_z == 0, lane % size_z == size_z - 1, lane < size_z, lane >= size_l - size_z

    def y_lower(a):
        _, _, y_first, _ = masks(a)
        inside = roll(a, size_z, 2)
        return jnp.where(y_first, roll(inside, 1, 0), inside)

    def y_upper(a):
        _, _, _, y_last = masks(a)
        inside = roll(a, -size_z, 2)
        return jnp.where(y_last, roll(inside, -1, 0), inside)

    def faces(k, scale):
        first, last, _, _ = masks(k[:, 1:-1])
        c = k[:, 1:-1]
        west_x = harmonic(k[:, :-2], c, scale)
        east_x = harmonic(c, k[:, 2:], scale)
        west_y = harmonic(y_lower(c), c, scale)
        east_y = harmonic(c, y_upper(c), scale)
        below = jnp.where(first, 2.0 * c * scale, harmonic(roll(c, 1, 2), c, scale))
        above = jnp.where(last, 2.0 * c * scale, harmonic(c, roll(c, -1, 2), scale))
        diagonal = west_x + east_x + west_y + east_y + below + above
        return (west_x, east_x, west_y, east_y, below, above, diagonal)

    def apply(v, faces):
        west_x, east_x, west_y, east_y, below, above, diagonal = faces
        c = v[:, 1:-1]
        first, last, _, _ = masks(c)
        under = jnp.where(first, 0.0, roll(c, 1, 2))
        over = jnp.where(last, 0.0, roll(c, -1, 2))
        beside_all = west_x * v[:, :-2] + east_x * v[:, 2:]
        beside_all = beside_all + west_y * y_lower(c) + east_y * y_upper(c)
        beside_all = beside_all + below * under + above * over
        return diagonal * c - beside_all

    return faces, apply


class LaneBand:
    def __init__(self, ops, k, scale, have, right_side, rhs_have):
        faces, self.apply = ops
        self.faces, self.have = faces(k, scale), have
        self.right_side, self.rhs_have = right_side, rhs_have

    def faces_at(self, h):
        t = self.have - h
        return tuple(f[:, t : f.shape[1] - t] for f in self.faces)

    def rhs_at(self, h):
        t = self.rhs_have - h
        return self.right_side[:, t : self.right_side.shape[1] - t]

    def sweep(self, v, h):
        faces = self.faces_at(h)
        residual = self.rhs_at(h) - self.apply(v, faces)
        return v[:, 1:-1] + OMEGA * residual / faces[6]

    def first_sweep(self, h):
        return OMEGA * self.rhs_at(h) / self.faces_at(h)[6]

    def residual(self, v):
        return self.rhs_at(0) - self.apply(v, self.faces_at(0))


def lane_pairs(size_y, size_z):
    n = size_y * size_z
    i = lax.broadcasted_iota(jnp.int32, (n, n // 4), 0)
    j = lax.broadcasted_iota(jnp.int32, (n, n // 4), 1)
    coarse = (i // size_z // 2) * (size_z // 2) + (i % size_z) // 2
    return (coarse == j).astype(jnp.float32)


def band_coarsen(field, size_y, size_z):
    t = along_y(field, pairs(field.shape[1]).T)
    t = jnp.einsum("cxl,lm->cxm", t, lane_pairs(size_y, size_z), precision=lax.Precision.HIGHEST)
    return t * 0.125


def band_prolong(field, size_y, size_z):
    t = jnp.einsum("cxm,lm->cxl", field, lane_pairs(size_y, size_z), precision=lax.Precision.HIGHEST)
    return along_y(t, pairs(2 * field.shape[1]))


def rows_halo(x, w, axis):
    size_x = x.shape[axis]
    lower = shift_from(lax.slice_in_dim(x, size_x - w, size_x, axis=axis), "row", 1)
    upper = shift_from(lax.slice_in_dim(x, 0, w, axis=axis), "row", -1)
    return jnp.concatenate([lower, x, upper], axis=axis)


def x_halo(x, w):
    size_x = x.shape[-3]
    lower = shift_from(x[..., size_x - w :, :, :], "row", 1)
    upper = shift_from(x[..., :w, :, :], "row", -1)
    return jnp.concatenate([lower, x, upper], axis=-3)


def rows_around(x, steps, axis):
    lower = [shift_from(x, "row", k) for k in reversed(steps)]
    upper = [shift_from(x, "row", -k) for k in steps]
    return jnp.concatenate(lower + [x] + upper, axis=axis)


def coarse_kernel(scale, size_z, spans, keep, lower_ref, own_ref, upper_ref, out_ref, tile_ref):
    span, extra = spans
    for f in range(2):
        tile_ref[f, 0:extra] = lower_ref[f]
        tile_ref[f, extra : extra + span] = own_ref[f]
        tile_ref[f, extra + span : 2 * extra + span] = upper_ref[f]
    b = tile_ref[0]
    k = tile_ref[1]
    rows, lanes = k.shape
    lane = lax.broadcasted_iota(jnp.int32, (rows, lanes), 1) % size_z
    first, last = lane == 0, lane == size_z - 1

    def x_lower(a):
        return pltpu.roll(a, 1, 0)

    def x_upper(a):
        return pltpu.roll(a, rows - 1, 0)

    def y_lower(a):
        return pltpu.roll(a, size_z, 1)

    def y_upper(a):
        return pltpu.roll(a, lanes - size_z, 1)

    def z_lower(a):
        return pltpu.roll(a, 1, 1)

    def z_upper(a):
        return pltpu.roll(a, lanes - 1, 1)

    west_x = harmonic(x_lower(k), k, scale)
    east_x = harmonic(k, x_upper(k), scale)
    west_y = harmonic(y_lower(k), k, scale)
    east_y = harmonic(k, y_upper(k), scale)
    below = jnp.where(first, 2.0 * k * scale, harmonic(z_lower(k), k, scale))
    above = jnp.where(last, 2.0 * k * scale, harmonic(k, z_upper(k), scale))
    diagonal = west_x + east_x + west_y + east_y + below + above

    def one_sweep(i, v):
        under = jnp.where(first, 0.0, z_lower(v))
        over = jnp.where(last, 0.0, z_upper(v))
        beside_all = west_x * x_lower(v) + east_x * x_upper(v)
        beside_all = beside_all + west_y * y_lower(v) + east_y * y_upper(v)
        beside_all = beside_all + below * under + above * over
        return v + OMEGA * (b - (diagonal * v - beside_all)) / diagonal

    v = OMEGA * b / diagonal
    v = lax.fori_loop(1, CSWEEPS, one_sweep, v)
    out_ref[...] = v[(rows - keep) // 2 : (rows + keep) // 2]


def coarse_solve(pair, size_z, scale):
    size_x, lanes = pair.shape[1:]
    near = rows_around(pair, (1, 2), 1)
    span = near.shape[1]
    extra = CSWEEPS + 2 - (span - size_x) // 2
    extra += (-(span + 2 * extra)) % 8 // 2
    assert 0 < extra <= span
    rows = span + 2 * extra
    keep = 8
    assert (rows - keep) // 2 >= CSWEEPS
    lower = shift_from(near[:, span - extra :], "row", 5)
    upper = shift_from(near[:, :extra], "row", -5)
    call = pl.pallas_call(
        lambda *refs: coarse_kernel(scale, size_z, (span, extra), keep, *refs),
        out_shape=jax.ShapeDtypeStruct((keep, lanes), jnp.float32),
        scratch_shapes=[pltpu.VMEM((2, rows, lanes), jnp.float32)],
        cost_estimate=pl.CostEstimate(
            flops=40 * CSWEEPS * rows * lanes, transcendentals=0, bytes_accessed=24 * rows * lanes
        ),
    )
    return call(lower, near, upper)


def on_device(pressure_in, source, permeability):
    scales = [0.25**level for level in range(LEVELS + 1)]
    k0, p0, b0 = halo(jnp.stack([permeability, pressure_in, source]), 4)
    lev0 = Level(faces_of(k0, scales[0]), 3, b0, 4)
    p = lev0.sweep(p0, 3)
    s0 = lev0.sweep(p, 2)
    rhs = coarsen(lev0.residual(trim(s0, 1)))
    perm = coarsen(permeability)
    k1, b1 = halo(jnp.stack([perm, rhs]), 5)
    lev1 = Level(faces_of(k1, scales[1]), 4, b1, 5)
    p = lev1.first_sweep(4)
    s1 = lev1.sweep(p, 3)
    rhs = coarsen(lev1.residual(trim(s1, 2)))
    perm = coarsen(perm)
    _, size_y2, size_z2 = rhs.shape
    block = jnp.stack([perm, rhs]).reshape(2, rhs.shape[0], size_y2 * size_z2)
    band = lax.all_gather(block, "col", axis=0, tiled=False)
    k2, b2 = jnp.moveaxis(rows_halo(band, 6, 2), 1, 0)
    ops = lane_band_ops(size_z2)
    lev2 = LaneBand(ops, k2, scales[2], 5, b2, 6)
    p = lev2.first_sweep(5)
    s2 = lev2.sweep(p, 4)
    rhs = band_coarsen(lev2.residual(s2[:, 3:-3]), size_y2, size_z2)
    perm = band_coarsen(band[:, 0], size_y2, size_z2)
    blocks, size_x3, lanes3 = rhs.shape
    pair = jnp.stack([rhs, perm], axis=1)
    pair = jnp.transpose(pair, (1, 2, 0, 3)).reshape(2, size_x3, blocks * lanes3)
    correction = coarse_solve(pair, size_z2 // 2, scales[3])
    correction = jnp.transpose(correction.reshape(-1, blocks, lanes3), (1, 0, 2))
    q = s2 + band_prolong(correction, size_y2, size_z2)
    q = lev2.sweep(q, 3)
    u2 = lev2.sweep(q, 2)
    u2 = jnp.concatenate([u2[-1:], u2, u2[:1]], axis=0)
    col = lax.axis_index("col")
    u2 = lax.dynamic_slice_in_dim(u2, col, 3, axis=0)
    edge = 2 * size_z2
    u2 = jnp.concatenate([u2[0, :, -edge:], u2[1], u2[2, :, :edge]], axis=1)
    u2 = u2.reshape(u2.shape[0], size_y2 + 4, size_z2)
    q = s1 + trim(prolong(u2), 1)
    q = lev1.sweep(q, 2)
    u1 = lev1.sweep(q, 1)
    q = s0 + prolong(u1)
    q = lev0.sweep(q, 1)
    return lev0.sweep(q, 0)


def solution(mesh):
    placed = (P("row", "col", None), P("row", "col", None), P("row", "col", None))
    return jax.shard_map(
        on_device, mesh=mesh, in_specs=placed, out_specs=P("row", "col", None), check_vma=False
    )
```

```python
import jax
import jax.numpy as jnp
from jax import lax
from jax.experimental import pallas as pl
from jax.experimental.pallas import tpu as pltpu
from jax.sharding import PartitionSpec as P

LEVELS = 3
NU1 = 2
NU2 = 2
CSWEEPS = 16

OMEGA = 0.8


def shift_from(x, axis, k):
    n = lax.axis_size(axis)
    return lax.ppermute(x, axis, [(i, (i + k) % n) for i in range(n)])


def halo(x, w):
    size_y = x.shape[-2]
    lower = shift_from(x[..., :, size_y - w :, :], "col", 1)
    upper = shift_from(x[..., :, :w, :], "col", -1)
    x = jnp.concatenate([lower, x, upper], axis=-2)
    size_x = x.shape[-3]
    lower = shift_from(x[..., size_x - w :, :, :], "row", 1)
    upper = shift_from(x[..., :w, :, :], "row", -1)
    return jnp.concatenate([lower, x, upper], axis=-3)


def trim(a, t, y=True):
    if t == 0:
        return a
    if y:
        return a[t:-t, t:-t]
    return a[t:-t]


def harmonic(left, right, scale):
    return 2.0 * left * right / (left + right) * scale


def faces_of(k, scale):
    c = k[1:-1, 1:-1]
    west_x = harmonic(k[:-2, 1:-1], c, scale)
    east_x = harmonic(c, k[2:, 1:-1], scale)
    west_y = harmonic(k[1:-1, :-2], c, scale)
    east_y = harmonic(c, k[1:-1, 2:], scale)
    inner = harmonic(c[:, :, :-1], c[:, :, 1:], scale)
    below = jnp.concatenate([2.0 * c[:, :, :1] * scale, inner], axis=2)
    above = jnp.concatenate([inner, 2.0 * c[:, :, -1:] * scale], axis=2)
    diagonal = west_x + east_x + west_y + east_y + below + above
    return (west_x, east_x, west_y, east_y, below, above, diagonal)


def apply_operator(v, faces):
    west_x, east_x, west_y, east_y, below, above, diagonal = faces
    c = v[1:-1, 1:-1]
    zero_plane = jnp.zeros_like(c[:, :, :1])
    under = jnp.concatenate([zero_plane, c[:, :, :-1]], axis=2)
    over = jnp.concatenate([c[:, :, 1:], zero_plane], axis=2)
    beside_all = west_x * v[:-2, 1:-1] + east_x * v[2:, 1:-1]
    beside_all = beside_all + west_y * v[1:-1, :-2] + east_y * v[1:-1, 2:]
    beside_all = beside_all + below * under + above * over
    return diagonal * c - beside_all


class Level:
    def __init__(self, faces, have, right_side, rhs_have):
        self.faces, self.have = faces, have
        self.right_side, self.rhs_have = right_side, rhs_have

    def faces_at(self, h, y=True):
        return tuple(trim(f, self.have - h, y) for f in self.faces)

    def rhs_at(self, h, y=True):
        return trim(self.right_side, self.rhs_have - h, y)

    def sweep(self, v, h):
        faces = self.faces_at(h)
        residual = self.rhs_at(h) - apply_operator(v, faces)
        return v[1:-1, 1:-1] + OMEGA * residual / faces[6]

    def first_sweep(self, h):
        return OMEGA * self.rhs_at(h) / self.faces_at(h)[6]

    def residual(self, v):
        return self.rhs_at(0) - apply_operator(v, self.faces_at(0))


def pairs(n):
    i = lax.broadcasted_iota(jnp.int32, (n, n // 2), 0)
    j = lax.broadcasted_iota(jnp.int32, (n, n // 2), 1)
    return (i // 2 == j).astype(jnp.float32)


def along_z(field, matrix):
    size_x, size_y, size_z = field.shape
    flat = field.reshape(size_x * size_y, size_z)
    out = jnp.dot(flat, matrix, precision=lax.Precision.HIGHEST)
    return out.reshape(size_x, size_y, matrix.shape[1])


def along_y(field, matrix):
    size_x = field.shape[0]
    batched = jnp.broadcast_to(matrix, (size_x,) + matrix.shape)
    return jnp.einsum("xjy,xyz->xjz", batched, field, precision=lax.Precision.HIGHEST)


def coarsen(field):
    size_x, size_y, size_z = field.shape
    t = field.reshape(size_x // 2, 2, size_y, size_z)
    t = t[:, 0] + t[:, 1]
    t = along_z(t, pairs(size_z))
    t = along_y(t, pairs(size_y).T)
    return t * 0.125


def prolong(field):
    size_x, size_y, size_z = field.shape
    t = along_z(field, pairs(2 * size_z).T)
    t = along_y(t, pairs(2 * size_y))
    t = jnp.broadcast_to(t[:, None], (size_x, 2) + t.shape[1:])
    return t.reshape(2 * size_x, 2 * size_y, 2 * size_z)


def wrap_y(a, w=1):
    return jnp.concatenate([a[:, -w:], a, a[:, :w]], axis=1)


def lane_band_ops(size_z):
    def roll(a, k, axis):
        return jnp.roll(a, k, axis=axis)

    def masks(a):
        lane = lax.broadcasted_iota(jnp.int32, a.shape, 2)
        size_l = a.shape[2]
        return lane % size_z == 0, lane % size_z == size_z - 1, lane < size_z, lane >= size_l - size_z

    def y_lower(a):
        _, _, y_first, _ = masks(a)
        inside = roll(a, size_z, 2)
        return jnp.where(y_first, roll(inside, 1, 0), inside)

    def y_upper(a):
        _, _, _, y_last = masks(a)
        inside = roll(a, -size_z, 2)
        return jnp.where(y_last, roll(inside, -1, 0), inside)

    def faces(k, scale):
        first, last, _, _ = masks(k[:, 1:-1])
        c = k[:, 1:-1]
        west_x = harmonic(k[:, :-2], c, scale)
        east_x = harmonic(c, k[:, 2:], scale)
        west_y = harmonic(y_lower(c), c, scale)
        east_y = harmonic(c, y_upper(c), scale)
        below = jnp.where(first, 2.0 * c * scale, harmonic(roll(c, 1, 2), c, scale))
        above = jnp.where(last, 2.0 * c * scale, harmonic(c, roll(c, -1, 2), scale))
        diagonal = west_x + east_x + west_y + east_y + below + above
        return (west_x, east_x, west_y, east_y, below, above, diagonal)

    def apply(v, faces):
        west_x, east_x, west_y, east_y, below, above, diagonal = faces
        c = v[:, 1:-1]
        first, last, _, _ = masks(c)
        under = jnp.where(first, 0.0, roll(c, 1, 2))
        over = jnp.where(last, 0.0, roll(c, -1, 2))
        beside_all = west_x * v[:, :-2] + east_x * v[:, 2:]
        beside_all = beside_all + west_y * y_lower(c) + east_y * y_upper(c)
        beside_all = beside_all + below * under + above * over
        return diagonal * c - beside_all

    return faces, apply


class LaneBand:
    def __init__(self, ops, k, scale, have, right_side, rhs_have):
        faces, self.apply = ops
        self.faces, self.have = faces(k, scale), have
        self.right_side, self.rhs_have = right_side, rhs_have

    def faces_at(self, h):
        t = self.have - h
        return tuple(f[:, t : f.shape[1] - t] for f in self.faces)

    def rhs_at(self, h):
        t = self.rhs_have - h
        return self.right_side[:, t : self.right_side.shape[1] - t]

    def sweep(self, v, h):
        faces = self.faces_at(h)
        residual = self.rhs_at(h) - self.apply(v, faces)
        return v[:, 1:-1] + OMEGA * residual / faces[6]

    def first_sweep(self, h):
        return OMEGA * self.rhs_at(h) / self.faces_at(h)[6]

    def residual(self, v):
        return self.rhs_at(0) - self.apply(v, self.faces_at(0))


def lane_pairs(size_y, size_z):
    n = size_y * size_z
    i = lax.broadcasted_iota(jnp.int32, (n, n // 4), 0)
    j = lax.broadcasted_iota(jnp.int32, (n, n // 4), 1)
    coarse = (i // size_z // 2) * (size_z // 2) + (i % size_z) // 2
    return (coarse == j).astype(jnp.float32)


def band_coarsen(field, size_y, size_z):
    t = along_y(field, pairs(field.shape[1]).T)
    t = jnp.einsum("cxl,lm->cxm", t, lane_pairs(size_y, size_z), precision=lax.Precision.HIGHEST)
    return t * 0.125


def band_prolong(field, size_y, size_z):
    t = jnp.einsum("cxm,lm->cxl", field, lane_pairs(size_y, size_z), precision=lax.Precision.HIGHEST)
    return along_y(t, pairs(2 * field.shape[1]))


def rows_halo(x, w, axis):
    size_x = x.shape[axis]
    lower = shift_from(lax.slice_in_dim(x, size_x - w, size_x, axis=axis), "row", 1)
    upper = shift_from(lax.slice_in_dim(x, 0, w, axis=axis), "row", -1)
    return jnp.concatenate([lower, x, upper], axis=axis)


def x_halo(x, w):
    size_x = x.shape[-3]
    lower = shift_from(x[..., size_x - w :, :, :], "row", 1)
    upper = shift_from(x[..., :w, :, :], "row", -1)
    return jnp.concatenate([lower, x, upper], axis=-3)


def rows_around(x, steps, axis):
    lower = [shift_from(x, "row", k) for k in reversed(steps)]
    upper = [shift_from(x, "row", -k) for k in steps]
    return jnp.concatenate(lower + [x] + upper, axis=axis)


def coarse_kernel(scale, size_z, keep, near_refs, lower_ref, upper_ref, out_ref, tile_ref):
    size_x = near_refs[0].shape[1]
    rows = tile_ref.shape[1]
    reach = (rows - size_x) // 2
    sources = [lower_ref.at[i] for i in range(3)] + list(near_refs) + [upper_ref.at[i] for i in range(3)]
    for d, ref in zip(range(-5, 6), sources):
        start = max(d * size_x, -reach)
        end = min(d * size_x + size_x, size_x + reach)
        if start >= end:
            continue
        for f in range(2):
            tile_ref[f, start + reach : end + reach] = ref[f, start - d * size_x : end - d * size_x]
    b = tile_ref[0]
    k = tile_ref[1]
    rows, lanes = k.shape
    lane = lax.broadcasted_iota(jnp.int32, (rows, lanes), 1) % size_z
    first, last = lane == 0, lane == size_z - 1

    def x_lower(a):
        return pltpu.roll(a, 1, 0)

    def x_upper(a):
        return pltpu.roll(a, rows - 1, 0)

    def y_lower(a):
        return pltpu.roll(a, size_z, 1)

    def y_upper(a):
        return pltpu.roll(a, lanes - size_z, 1)

    def z_lower(a):
        return pltpu.roll(a, 1, 1)

    def z_upper(a):
        return pltpu.roll(a, lanes - 1, 1)

    west_x = harmonic(x_lower(k), k, scale)
    east_x = harmonic(k, x_upper(k), scale)
    west_y = harmonic(y_lower(k), k, scale)
    east_y = harmonic(k, y_upper(k), scale)
    below = jnp.where(first, 2.0 * k * scale, harmonic(z_lower(k), k, scale))
    above = jnp.where(last, 2.0 * k * scale, harmonic(k, z_upper(k), scale))
    diagonal = west_x + east_x + west_y + east_y + below + above

    def one_sweep(i, v):
        under = jnp.where(first, 0.0, z_lower(v))
        over = jnp.where(last, 0.0, z_upper(v))
        beside_all = west_x * x_lower(v) + east_x * x_upper(v)
        beside_all = beside_all + west_y * y_lower(v) + east_y * y_upper(v)
        beside_all = beside_all + below * under + above * over
        return v + OMEGA * (b - (diagonal * v - beside_all)) / diagonal

    v = OMEGA * b / diagonal
    v = lax.fori_loop(1, CSWEEPS, one_sweep, v)
    out_ref[...] = v[(rows - keep) // 2 : (rows + keep) // 2]


def coarse_solve(pair, size_z, scale):
    size_x, lanes = pair.shape[1:]
    m1, p1 = shift_from(pair, "row", 1), shift_from(pair, "row", -1)
    m2, p2 = shift_from(pair, "row", 2), shift_from(pair, "row", -2)
    near = [m2, m1, pair, p1, p2]
    lower = shift_from(jnp.stack([pair, p1, p2]), "row", 5)
    upper = shift_from(jnp.stack([m2, m1, pair]), "row", -5)
    reach = CSWEEPS + 2
    reach += (-(size_x + 2 * reach)) % 8 // 2
    assert reach <= 5 * size_x
    rows = size_x + 2 * reach
    keep = 8
    assert (rows - keep) // 2 >= CSWEEPS
    call = pl.pallas_call(
        lambda *refs: coarse_kernel(scale, size_z, keep, refs[:5], *refs[5:]),
        out_shape=jax.ShapeDtypeStruct((keep, lanes), jnp.float32),
        scratch_shapes=[pltpu.VMEM((2, rows, lanes), jnp.float32)],
        cost_estimate=pl.CostEstimate(
            flops=40 * CSWEEPS * rows * lanes, transcendentals=0, bytes_accessed=24 * rows * lanes
        ),
    )
    return call(*near, lower, upper)


def on_device(pressure_in, source, permeability):
    scales = [0.25**level for level in range(LEVELS + 1)]
    k0, p0, b0 = halo(jnp.stack([permeability, pressure_in, source]), 4)
    lev0 = Level(faces_of(k0, scales[0]), 3, b0, 4)
    p = lev0.sweep(p0, 3)
    s0 = lev0.sweep(p, 2)
    rhs = coarsen(lev0.residual(trim(s0, 1)))
    perm = coarsen(permeability)
    k1, b1 = halo(jnp.stack([perm, rhs]), 5)
    lev1 = Level(faces_of(k1, scales[1]), 4, b1, 5)
    p = lev1.first_sweep(4)
    s1 = lev1.sweep(p, 3)
    rhs = coarsen(lev1.residual(trim(s1, 2)))
    perm = coarsen(perm)
    _, size_y2, size_z2 = rhs.shape
    block = jnp.stack([perm, rhs]).reshape(2, rhs.shape[0], size_y2 * size_z2)
    band = lax.all_gather(block, "col", axis=0, tiled=False)
    k2, b2 = jnp.moveaxis(rows_halo(band, 6, 2), 1, 0)
    ops = lane_band_ops(size_z2)
    lev2 = LaneBand(ops, k2, scales[2], 5, b2, 6)
    p = lev2.first_sweep(5)
    s2 = lev2.sweep(p, 4)
    rhs = band_coarsen(lev2.residual(s2[:, 3:-3]), size_y2, size_z2)
    perm = band_coarsen(band[:, 0], size_y2, size_z2)
    blocks, size_x3, lanes3 = rhs.shape
    pair = jnp.stack([rhs, perm], axis=1)
    pair = jnp.transpose(pair, (1, 2, 0, 3)).reshape(2, size_x3, blocks * lanes3)
    correction = coarse_solve(pair, size_z2 // 2, scales[3])
    correction = jnp.transpose(correction.reshape(-1, blocks, lanes3), (1, 0, 2))
    q = s2 + band_prolong(correction, size_y2, size_z2)
    q = lev2.sweep(q, 3)
    u2 = lev2.sweep(q, 2)
    u2 = jnp.concatenate([u2[-1:], u2, u2[:1]], axis=0)
    col = lax.axis_index("col")
    u2 = lax.dynamic_slice_in_dim(u2, col, 3, axis=0)
    edge = 2 * size_z2
    u2 = jnp.concatenate([u2[0, :, -edge:], u2[1], u2[2, :, :edge]], axis=1)
    u2 = u2.reshape(u2.shape[0], size_y2 + 4, size_z2)
    q = s1 + trim(prolong(u2), 1)
    q = lev1.sweep(q, 2)
    u1 = lev1.sweep(q, 1)
    q = s0 + prolong(u1)
    q = lev0.sweep(q, 1)
    return lev0.sweep(q, 0)


def solution(mesh):
    placed = (P("row", "col", None), P("row", "col", None), P("row", "col", None))
    return jax.shard_map(
        on_device, mesh=mesh, in_specs=placed, out_specs=P("row", "col", None), check_vma=False
    )
```

```python
import jax
import jax.numpy as jnp
from jax import lax
from jax.experimental import pallas as pl
from jax.experimental.pallas import tpu as pltpu
from jax.sharding import PartitionSpec as P

LEVELS = 3
NU1 = 2
NU2 = 2
CSWEEPS = 16

OMEGA = 0.8


def shift_from(x, axis, k):
    n = lax.axis_size(axis)
    return lax.ppermute(x, axis, [(i, (i + k) % n) for i in range(n)])


def halo(x, w):
    size_y = x.shape[-2]
    lower = shift_from(x[..., :, size_y - w :, :], "col", 1)
    upper = shift_from(x[..., :, :w, :], "col", -1)
    x = jnp.concatenate([lower, x, upper], axis=-2)
    size_x = x.shape[-3]
    lower = shift_from(x[..., size_x - w :, :, :], "row", 1)
    upper = shift_from(x[..., :w, :, :], "row", -1)
    return jnp.concatenate([lower, x, upper], axis=-3)


def trim(a, t, y=True):
    if t == 0:
        return a
    if y:
        return a[t:-t, t:-t]
    return a[t:-t]


def harmonic(left, right, scale):
    return 2.0 * left * right / (left + right) * scale


def faces_of(k, scale):
    c = k[1:-1, 1:-1]
    west_x = harmonic(k[:-2, 1:-1], c, scale)
    east_x = harmonic(c, k[2:, 1:-1], scale)
    west_y = harmonic(k[1:-1, :-2], c, scale)
    east_y = harmonic(c, k[1:-1, 2:], scale)
    inner = harmonic(c[:, :, :-1], c[:, :, 1:], scale)
    below = jnp.concatenate([2.0 * c[:, :, :1] * scale, inner], axis=2)
    above = jnp.concatenate([inner, 2.0 * c[:, :, -1:] * scale], axis=2)
    diagonal = west_x + east_x + west_y + east_y + below + above
    return (west_x, east_x, west_y, east_y, below, above, diagonal)


def apply_operator(v, faces):
    west_x, east_x, west_y, east_y, below, above, diagonal = faces
    c = v[1:-1, 1:-1]
    zero_plane = jnp.zeros_like(c[:, :, :1])
    under = jnp.concatenate([zero_plane, c[:, :, :-1]], axis=2)
    over = jnp.concatenate([c[:, :, 1:], zero_plane], axis=2)
    beside_all = west_x * v[:-2, 1:-1] + east_x * v[2:, 1:-1]
    beside_all = beside_all + west_y * v[1:-1, :-2] + east_y * v[1:-1, 2:]
    beside_all = beside_all + below * under + above * over
    return diagonal * c - beside_all


class Level:
    def __init__(self, faces, have, right_side, rhs_have):
        self.faces, self.have = faces, have
        self.right_side, self.rhs_have = right_side, rhs_have

    def faces_at(self, h, y=True):
        return tuple(trim(f, self.have - h, y) for f in self.faces)

    def rhs_at(self, h, y=True):
        return trim(self.right_side, self.rhs_have - h, y)

    def sweep(self, v, h):
        faces = self.faces_at(h)
        residual = self.rhs_at(h) - apply_operator(v, faces)
        return v[1:-1, 1:-1] + OMEGA * residual / faces[6]

    def first_sweep(self, h):
        return OMEGA * self.rhs_at(h) / self.faces_at(h)[6]

    def residual(self, v):
        return self.rhs_at(0) - apply_operator(v, self.faces_at(0))


def pairs(n):
    i = lax.broadcasted_iota(jnp.int32, (n, n // 2), 0)
    j = lax.broadcasted_iota(jnp.int32, (n, n // 2), 1)
    return (i // 2 == j).astype(jnp.float32)


def along_z(field, matrix):
    size_x, size_y, size_z = field.shape
    flat = field.reshape(size_x * size_y, size_z)
    out = jnp.dot(flat, matrix, precision=lax.Precision.HIGHEST)
    return out.reshape(size_x, size_y, matrix.shape[1])


def along_y(field, matrix):
    size_x = field.shape[0]
    batched = jnp.broadcast_to(matrix, (size_x,) + matrix.shape)
    return jnp.einsum("xjy,xyz->xjz", batched, field, precision=lax.Precision.HIGHEST)


def coarsen(field):
    size_x, size_y, size_z = field.shape
    t = field.reshape(size_x // 2, 2, size_y, size_z)
    t = t[:, 0] + t[:, 1]
    t = along_z(t, pairs(size_z))
    t = along_y(t, pairs(size_y).T)
    return t * 0.125


def prolong(field):
    size_x, size_y, size_z = field.shape
    t = along_z(field, pairs(2 * size_z).T)
    t = along_y(t, pairs(2 * size_y))
    t = jnp.broadcast_to(t[:, None], (size_x, 2) + t.shape[1:])
    return t.reshape(2 * size_x, 2 * size_y, 2 * size_z)


def wrap_y(a, w=1):
    return jnp.concatenate([a[:, -w:], a, a[:, :w]], axis=1)


def lane_band_ops(size_z):
    def roll(a, k, axis):
        return jnp.roll(a, k, axis=axis)

    def masks(a):
        lane = lax.broadcasted_iota(jnp.int32, a.shape, 2)
        size_l = a.shape[2]
        return lane % size_z == 0, lane % size_z == size_z - 1, lane < size_z, lane >= size_l - size_z

    def y_lower(a):
        _, _, y_first, _ = masks(a)
        inside = roll(a, size_z, 2)
        return jnp.where(y_first, roll(inside, 1, 0), inside)

    def y_upper(a):
        _, _, _, y_last = masks(a)
        inside = roll(a, -size_z, 2)
        return jnp.where(y_last, roll(inside, -1, 0), inside)

    def faces(k, scale):
        first, last, _, _ = masks(k[:, 1:-1])
        c = k[:, 1:-1]
        west_x = harmonic(k[:, :-2], c, scale)
        east_x = harmonic(c, k[:, 2:], scale)
        west_y = harmonic(y_lower(c), c, scale)
        east_y = harmonic(c, y_upper(c), scale)
        below = jnp.where(first, 2.0 * c * scale, harmonic(roll(c, 1, 2), c, scale))
        above = jnp.where(last, 2.0 * c * scale, harmonic(c, roll(c, -1, 2), scale))
        diagonal = west_x + east_x + west_y + east_y + below + above
        return (west_x, east_x, west_y, east_y, below, above, diagonal)

    def apply(v, faces):
        west_x, east_x, west_y, east_y, below, above, diagonal = faces
        c = v[:, 1:-1]
        first, last, _, _ = masks(c)
        under = jnp.where(first, 0.0, roll(c, 1, 2))
        over = jnp.where(last, 0.0, roll(c, -1, 2))
        beside_all = west_x * v[:, :-2] + east_x * v[:, 2:]
        beside_all = beside_all + west_y * y_lower(c) + east_y * y_upper(c)
        beside_all = beside_all + below * under + above * over
        return diagonal * c - beside_all

    return faces, apply


class LaneBand:
    def __init__(self, ops, k, scale, have, right_side, rhs_have):
        faces, self.apply = ops
        self.faces, self.have = faces(k, scale), have
        self.right_side, self.rhs_have = right_side, rhs_have

    def faces_at(self, h):
        t = self.have - h
        return tuple(f[:, t : f.shape[1] - t] for f in self.faces)

    def rhs_at(self, h):
        t = self.rhs_have - h
        return self.right_side[:, t : self.right_side.shape[1] - t]

    def sweep(self, v, h):
        faces = self.faces_at(h)
        residual = self.rhs_at(h) - self.apply(v, faces)
        return v[:, 1:-1] + OMEGA * residual / faces[6]

    def first_sweep(self, h):
        return OMEGA * self.rhs_at(h) / self.faces_at(h)[6]

    def residual(self, v):
        return self.rhs_at(0) - self.apply(v, self.faces_at(0))


def lane_pairs(size_y, size_z):
    n = size_y * size_z
    i = lax.broadcasted_iota(jnp.int32, (n, n // 4), 0)
    j = lax.broadcasted_iota(jnp.int32, (n, n // 4), 1)
    coarse = (i // size_z // 2) * (size_z // 2) + (i % size_z) // 2
    return (coarse == j).astype(jnp.float32)


def band_coarsen(field, size_y, size_z):
    t = along_y(field, pairs(field.shape[1]).T)
    t = jnp.einsum("cxl,lm->cxm", t, lane_pairs(size_y, size_z), precision=lax.Precision.HIGHEST)
    return t * 0.125


def band_prolong(field, size_y, size_z):
    t = jnp.einsum("cxm,lm->cxl", field, lane_pairs(size_y, size_z), precision=lax.Precision.HIGHEST)
    return along_y(t, pairs(2 * field.shape[1]))


def rows_halo(x, w, axis):
    size_x = x.shape[axis]
    lower = shift_from(lax.slice_in_dim(x, size_x - w, size_x, axis=axis), "row", 1)
    upper = shift_from(lax.slice_in_dim(x, 0, w, axis=axis), "row", -1)
    return jnp.concatenate([lower, x, upper], axis=axis)


def x_halo(x, w):
    size_x = x.shape[-3]
    lower = shift_from(x[..., size_x - w :, :, :], "row", 1)
    upper = shift_from(x[..., :w, :, :], "row", -1)
    return jnp.concatenate([lower, x, upper], axis=-3)


def rows_around(x, steps, axis):
    lower = [shift_from(x, "row", k) for k in reversed(steps)]
    upper = [shift_from(x, "row", -k) for k in steps]
    return jnp.concatenate(lower + [x] + upper, axis=axis)


def coarse_kernel(scale, size_z, keep, near_refs, lower_ref, upper_ref, out_ref, tile_ref):
    size_x = near_refs[0].shape[1]
    rows = tile_ref.shape[1]
    reach = (rows - size_x) // 2
    sources = [lower_ref.at[i] for i in range(3)] + list(near_refs) + [upper_ref.at[i] for i in range(3)]
    for d, ref in zip(range(-5, 6), sources):
        start = max(d * size_x, -reach)
        end = min(d * size_x + size_x, size_x + reach)
        if start >= end:
            continue
        for f in range(2):
            tile_ref[f, start + reach : end + reach] = ref[f, start - d * size_x : end - d * size_x]
    b = tile_ref[0]
    k = tile_ref[1]
    rows, lanes = k.shape
    lane = lax.broadcasted_iota(jnp.int32, (rows, lanes), 1) % size_z
    first, last = lane == 0, lane == size_z - 1

    def x_lower(a):
        return pltpu.roll(a, 1, 0)

    def x_upper(a):
        return pltpu.roll(a, rows - 1, 0)

    def y_lower(a):
        return pltpu.roll(a, size_z, 1)

    def y_upper(a):
        return pltpu.roll(a, lanes - size_z, 1)

    def z_lower(a):
        return pltpu.roll(a, 1, 1)

    def z_upper(a):
        return pltpu.roll(a, lanes - 1, 1)

    west_x = harmonic(x_lower(k), k, scale)
    east_x = harmonic(k, x_upper(k), scale)
    west_y = harmonic(y_lower(k), k, scale)
    east_y = harmonic(k, y_upper(k), scale)
    below = jnp.where(first, 2.0 * k * scale, harmonic(z_lower(k), k, scale))
    above = jnp.where(last, 2.0 * k * scale, harmonic(k, z_upper(k), scale))
    diagonal = west_x + east_x + west_y + east_y + below + above

    def one_sweep(i, v):
        under = jnp.where(first, 0.0, z_lower(v))
        over = jnp.where(last, 0.0, z_upper(v))
        beside_all = west_x * x_lower(v) + east_x * x_upper(v)
        beside_all = beside_all + west_y * y_lower(v) + east_y * y_upper(v)
        beside_all = beside_all + below * under + above * over
        return v + OMEGA * (b - (diagonal * v - beside_all)) / diagonal

    v = OMEGA * b / diagonal
    v = lax.fori_loop(1, CSWEEPS, one_sweep, v)
    out_ref[...] = v[(rows - keep) // 2 : (rows + keep) // 2]


def coarse_solve(pair, size_z, scale):
    size_x, lanes = pair.shape[1:]
    m1, p1 = shift_from(pair, "row", 1), shift_from(pair, "row", -1)
    m2, p2 = shift_from(pair, "row", 2), shift_from(pair, "row", -2)
    near = [m2, m1, pair, p1, p2]
    lower = shift_from(jnp.stack([m2, m1, pair]), "row", 3)
    upper = shift_from(jnp.stack([pair, p1, p2]), "row", -3)
    reach = CSWEEPS + 2
    reach += (-(size_x + 2 * reach)) % 8 // 2
    assert reach <= 5 * size_x
    rows = size_x + 2 * reach
    keep = 8
    assert (rows - keep) // 2 >= CSWEEPS
    call = pl.pallas_call(
        lambda *refs: coarse_kernel(scale, size_z, keep, refs[:5], *refs[5:]),
        out_shape=jax.ShapeDtypeStruct((keep, lanes), jnp.float32),
        scratch_shapes=[pltpu.VMEM((2, rows, lanes), jnp.float32)],
        cost_estimate=pl.CostEstimate(
            flops=40 * CSWEEPS * rows * lanes, transcendentals=0, bytes_accessed=24 * rows * lanes
        ),
    )
    return call(*near, lower, upper)


def on_device(pressure_in, source, permeability):
    scales = [0.25**level for level in range(LEVELS + 1)]
    k0, p0, b0 = halo(jnp.stack([permeability, pressure_in, source]), 4)
    lev0 = Level(faces_of(k0, scales[0]), 3, b0, 4)
    p = lev0.sweep(p0, 3)
    s0 = lev0.sweep(p, 2)
    rhs = coarsen(lev0.residual(trim(s0, 1)))
    perm = coarsen(permeability)
    k1, b1 = halo(jnp.stack([perm, rhs]), 5)
    lev1 = Level(faces_of(k1, scales[1]), 4, b1, 5)
    p = lev1.first_sweep(4)
    s1 = lev1.sweep(p, 3)
    rhs = coarsen(lev1.residual(trim(s1, 2)))
    perm = coarsen(perm)
    _, size_y2, size_z2 = rhs.shape
    block = jnp.stack([perm, rhs]).reshape(2, rhs.shape[0], size_y2 * size_z2)
    band = lax.all_gather(block, "col", axis=0, tiled=False)
    k2, b2 = jnp.moveaxis(rows_halo(band, 6, 2), 1, 0)
    ops = lane_band_ops(size_z2)
    lev2 = LaneBand(ops, k2, scales[2], 5, b2, 6)
    p = lev2.first_sweep(5)
    s2 = lev2.sweep(p, 4)
    rhs = band_coarsen(lev2.residual(s2[:, 3:-3]), size_y2, size_z2)
    perm = band_coarsen(band[:, 0], size_y2, size_z2)
    blocks, size_x3, lanes3 = rhs.shape
    pair = jnp.stack([rhs, perm], axis=1)
    pair = jnp.transpose(pair, (1, 2, 0, 3)).reshape(2, size_x3, blocks * lanes3)
    correction = coarse_solve(pair, size_z2 // 2, scales[3])
    correction = jnp.transpose(correction.reshape(-1, blocks, lanes3), (1, 0, 2))
    q = s2 + band_prolong(correction, size_y2, size_z2)
    q = lev2.sweep(q, 3)
    u2 = lev2.sweep(q, 2)
    u2 = jnp.concatenate([u2[-1:], u2, u2[:1]], axis=0)
    col = lax.axis_index("col")
    u2 = lax.dynamic_slice_in_dim(u2, col, 3, axis=0)
    edge = 2 * size_z2
    u2 = jnp.concatenate([u2[0, :, -edge:], u2[1], u2[2, :, :edge]], axis=1)
    u2 = u2.reshape(u2.shape[0], size_y2 + 4, size_z2)
    q = s1 + trim(prolong(u2), 1)
    q = lev1.sweep(q, 2)
    u1 = lev1.sweep(q, 1)
    q = s0 + prolong(u1)
    q = lev0.sweep(q, 1)
    return lev0.sweep(q, 0)


def solution(mesh):
    placed = (P("row", "col", None), P("row", "col", None), P("row", "col", None))
    return jax.shard_map(
        on_device, mesh=mesh, in_specs=placed, out_specs=P("row", "col", None), check_vma=False
    )
```

```python
import jax
import jax.numpy as jnp
from jax import lax
from jax.experimental import pallas as pl
from jax.experimental.pallas import tpu as pltpu
from jax.sharding import PartitionSpec as P

LEVELS = 3
NU1 = 2
NU2 = 2
CSWEEPS = 16

OMEGA = 0.8


def shift_from(x, axis, k):
    n = lax.axis_size(axis)
    return lax.ppermute(x, axis, [(i, (i + k) % n) for i in range(n)])


def halo(x, w):
    size_y = x.shape[-2]
    lower = shift_from(x[..., :, size_y - w :, :], "col", 1)
    upper = shift_from(x[..., :, :w, :], "col", -1)
    x = jnp.concatenate([lower, x, upper], axis=-2)
    size_x = x.shape[-3]
    lower = shift_from(x[..., size_x - w :, :, :], "row", 1)
    upper = shift_from(x[..., :w, :, :], "row", -1)
    return jnp.concatenate([lower, x, upper], axis=-3)


def trim(a, t, y=True):
    if t == 0:
        return a
    if y:
        return a[t:-t, t:-t]
    return a[t:-t]


def harmonic(left, right, scale):
    return 2.0 * left * right / (left + right) * scale


def faces_of(k, scale):
    c = k[1:-1, 1:-1]
    west_x = harmonic(k[:-2, 1:-1], c, scale)
    east_x = harmonic(c, k[2:, 1:-1], scale)
    west_y = harmonic(k[1:-1, :-2], c, scale)
    east_y = harmonic(c, k[1:-1, 2:], scale)
    inner = harmonic(c[:, :, :-1], c[:, :, 1:], scale)
    below = jnp.concatenate([2.0 * c[:, :, :1] * scale, inner], axis=2)
    above = jnp.concatenate([inner, 2.0 * c[:, :, -1:] * scale], axis=2)
    diagonal = west_x + east_x + west_y + east_y + below + above
    return (west_x, east_x, west_y, east_y, below, above, diagonal)


def apply_operator(v, faces):
    west_x, east_x, west_y, east_y, below, above, diagonal = faces
    c = v[1:-1, 1:-1]
    zero_plane = jnp.zeros_like(c[:, :, :1])
    under = jnp.concatenate([zero_plane, c[:, :, :-1]], axis=2)
    over = jnp.concatenate([c[:, :, 1:], zero_plane], axis=2)
    beside_all = west_x * v[:-2, 1:-1] + east_x * v[2:, 1:-1]
    beside_all = beside_all + west_y * v[1:-1, :-2] + east_y * v[1:-1, 2:]
    beside_all = beside_all + below * under + above * over
    return diagonal * c - beside_all


class Level:
    def __init__(self, faces, have, right_side, rhs_have):
        self.faces, self.have = faces, have
        self.right_side, self.rhs_have = right_side, rhs_have

    def faces_at(self, h, y=True):
        return tuple(trim(f, self.have - h, y) for f in self.faces)

    def rhs_at(self, h, y=True):
        return trim(self.right_side, self.rhs_have - h, y)

    def sweep(self, v, h):
        faces = self.faces_at(h)
        residual = self.rhs_at(h) - apply_operator(v, faces)
        return v[1:-1, 1:-1] + OMEGA * residual / faces[6]

    def first_sweep(self, h):
        return OMEGA * self.rhs_at(h) / self.faces_at(h)[6]

    def residual(self, v):
        return self.rhs_at(0) - apply_operator(v, self.faces_at(0))


def pairs(n):
    i = lax.broadcasted_iota(jnp.int32, (n, n // 2), 0)
    j = lax.broadcasted_iota(jnp.int32, (n, n // 2), 1)
    return (i // 2 == j).astype(jnp.float32)


def along_z(field, matrix):
    size_x, size_y, size_z = field.shape
    flat = field.reshape(size_x * size_y, size_z)
    out = jnp.dot(flat, matrix, precision=lax.Precision.HIGHEST)
    return out.reshape(size_x, size_y, matrix.shape[1])


def along_y(field, matrix):
    size_x = field.shape[0]
    batched = jnp.broadcast_to(matrix, (size_x,) + matrix.shape)
    return jnp.einsum("xjy,xyz->xjz", batched, field, precision=lax.Precision.HIGHEST)


def coarsen(field):
    size_x, size_y, size_z = field.shape
    t = field.reshape(size_x // 2, 2, size_y, size_z)
    t = t[:, 0] + t[:, 1]
    t = along_z(t, pairs(size_z))
    t = along_y(t, pairs(size_y).T)
    return t * 0.125


def prolong(field):
    size_x, size_y, size_z = field.shape
    t = along_z(field, pairs(2 * size_z).T)
    t = along_y(t, pairs(2 * size_y))
    t = jnp.broadcast_to(t[:, None], (size_x, 2) + t.shape[1:])
    return t.reshape(2 * size_x, 2 * size_y, 2 * size_z)


def wrap_y(a, w=1):
    return jnp.concatenate([a[:, -w:], a, a[:, :w]], axis=1)


def lane_band_ops(size_z):
    def roll(a, k, axis):
        return jnp.roll(a, k, axis=axis)

    def masks(a):
        lane = lax.broadcasted_iota(jnp.int32, a.shape, 2)
        size_l = a.shape[2]
        return lane % size_z == 0, lane % size_z == size_z - 1, lane < size_z, lane >= size_l - size_z

    def y_lower(a):
        _, _, y_first, _ = masks(a)
        inside = roll(a, size_z, 2)
        return jnp.where(y_first, roll(inside, 1, 0), inside)

    def y_upper(a):
        _, _, _, y_last = masks(a)
        inside = roll(a, -size_z, 2)
        return jnp.where(y_last, roll(inside, -1, 0), inside)

    def faces(k, scale):
        first, last, _, _ = masks(k[:, 1:-1])
        c = k[:, 1:-1]
        west_x = harmonic(k[:, :-2], c, scale)
        east_x = harmonic(c, k[:, 2:], scale)
        west_y = harmonic(y_lower(c), c, scale)
        east_y = harmonic(c, y_upper(c), scale)
        below = jnp.where(first, 2.0 * c * scale, harmonic(roll(c, 1, 2), c, scale))
        above = jnp.where(last, 2.0 * c * scale, harmonic(c, roll(c, -1, 2), scale))
        diagonal = west_x + east_x + west_y + east_y + below + above
        return (west_x, east_x, west_y, east_y, below, above, diagonal)

    def apply(v, faces):
        west_x, east_x, west_y, east_y, below, above, diagonal = faces
        c = v[:, 1:-1]
        first, last, _, _ = masks(c)
        under = jnp.where(first, 0.0, roll(c, 1, 2))
        over = jnp.where(last, 0.0, roll(c, -1, 2))
        beside_all = west_x * v[:, :-2] + east_x * v[:, 2:]
        beside_all = beside_all + west_y * y_lower(c) + east_y * y_upper(c)
        beside_all = beside_all + below * under + above * over
        return diagonal * c - beside_all

    return faces, apply


class LaneBand:
    def __init__(self, ops, k, scale, have, right_side, rhs_have):
        faces, self.apply = ops
        self.faces, self.have = faces(k, scale), have
        self.right_side, self.rhs_have = right_side, rhs_have

    def faces_at(self, h):
        t = self.have - h
        return tuple(f[:, t : f.shape[1] - t] for f in self.faces)

    def rhs_at(self, h):
        t = self.rhs_have - h
        return self.right_side[:, t : self.right_side.shape[1] - t]

    def sweep(self, v, h):
        faces = self.faces_at(h)
        residual = self.rhs_at(h) - self.apply(v, faces)
        return v[:, 1:-1] + OMEGA * residual / faces[6]

    def first_sweep(self, h):
        return OMEGA * self.rhs_at(h) / self.faces_at(h)[6]

    def residual(self, v):
        return self.rhs_at(0) - self.apply(v, self.faces_at(0))


def lane_pairs(size_y, size_z):
    n = size_y * size_z
    i = lax.broadcasted_iota(jnp.int32, (n, n // 4), 0)
    j = lax.broadcasted_iota(jnp.int32, (n, n // 4), 1)
    coarse = (i // size_z // 2) * (size_z // 2) + (i % size_z) // 2
    return (coarse == j).astype(jnp.float32)


def band_coarsen(field, size_y, size_z):
    t = along_y(field, pairs(field.shape[1]).T)
    t = jnp.einsum("cxl,lm->cxm", t, lane_pairs(size_y, size_z), precision=lax.Precision.HIGHEST)
    return t * 0.125


def band_prolong(field, size_y, size_z):
    t = jnp.einsum("cxm,lm->cxl", field, lane_pairs(size_y, size_z), precision=lax.Precision.HIGHEST)
    return along_y(t, pairs(2 * field.shape[1]))


def rows_halo(x, w, axis):
    size_x = x.shape[axis]
    lower = shift_from(lax.slice_in_dim(x, size_x - w, size_x, axis=axis), "row", 1)
    upper = shift_from(lax.slice_in_dim(x, 0, w, axis=axis), "row", -1)
    return jnp.concatenate([lower, x, upper], axis=axis)


def x_halo(x, w):
    size_x = x.shape[-3]
    lower = shift_from(x[..., size_x - w :, :, :], "row", 1)
    upper = shift_from(x[..., :w, :, :], "row", -1)
    return jnp.concatenate([lower, x, upper], axis=-3)


def rows_around(x, steps, axis):
    lower = [shift_from(x, "row", k) for k in reversed(steps)]
    upper = [shift_from(x, "row", -k) for k in steps]
    return jnp.concatenate(lower + [x] + upper, axis=axis)


def coarse_kernel(scale, size_z, keep, near_refs, lower_ref, upper_ref, out_ref, tile_ref):
    size_x = near_refs[0].shape[1]
    rows = tile_ref.shape[1]
    reach = (rows - size_x) // 2
    sources = [lower_ref.at[i] for i in range(3)] + list(near_refs) + [upper_ref.at[i] for i in range(3)]
    for d, ref in zip(range(-5, 6), sources):
        start = max(d * size_x, -reach)
        end = min(d * size_x + size_x, size_x + reach)
        if start >= end:
            continue
        for f in range(2):
            tile_ref[f, start + reach : end + reach] = ref[f, start - d * size_x : end - d * size_x]
    b = tile_ref[0]
    k = tile_ref[1]
    rows, lanes = k.shape
    lane = lax.broadcasted_iota(jnp.int32, (rows, lanes), 1) % size_z
    first, last = lane == 0, lane == size_z - 1

    def x_lower(a):
        return pltpu.roll(a, 1, 0)

    def x_upper(a):
        return pltpu.roll(a, rows - 1, 0)

    def y_lower(a):
        return pltpu.roll(a, size_z, 1)

    def y_upper(a):
        return pltpu.roll(a, lanes - size_z, 1)

    def z_lower(a):
        return pltpu.roll(a, 1, 1)

    def z_upper(a):
        return pltpu.roll(a, lanes - 1, 1)

    west_x = harmonic(x_lower(k), k, scale)
    east_x = harmonic(k, x_upper(k), scale)
    west_y = harmonic(y_lower(k), k, scale)
    east_y = harmonic(k, y_upper(k), scale)
    below = jnp.where(first, 2.0 * k * scale, harmonic(z_lower(k), k, scale))
    above = jnp.where(last, 2.0 * k * scale, harmonic(k, z_upper(k), scale))
    diagonal = west_x + east_x + west_y + east_y + below + above

    def one_sweep(i, v):
        under = jnp.where(first, 0.0, z_lower(v))
        over = jnp.where(last, 0.0, z_upper(v))
        beside_all = west_x * x_lower(v) + east_x * x_upper(v)
        beside_all = beside_all + west_y * y_lower(v) + east_y * y_upper(v)
        beside_all = beside_all + below * under + above * over
        return v + OMEGA * (b - (diagonal * v - beside_all)) / diagonal

    v = OMEGA * b / diagonal
    v = lax.fori_loop(1, CSWEEPS, one_sweep, v, unroll=True)
    out_ref[...] = v[(rows - keep) // 2 : (rows + keep) // 2]


def coarse_solve(pair, size_z, scale):
    size_x, lanes = pair.shape[1:]
    m1, p1 = shift_from(pair, "row", 1), shift_from(pair, "row", -1)
    m2, p2 = shift_from(pair, "row", 2), shift_from(pair, "row", -2)
    near = [m2, m1, pair, p1, p2]
    lower = shift_from(jnp.stack([m2, m1, pair]), "row", 3)
    upper = shift_from(jnp.stack([pair, p1, p2]), "row", -3)
    reach = CSWEEPS + 2
    reach += (-(size_x + 2 * reach)) % 8 // 2
    assert reach <= 5 * size_x
    rows = size_x + 2 * reach
    keep = 8
    assert (rows - keep) // 2 >= CSWEEPS
    call = pl.pallas_call(
        lambda *refs: coarse_kernel(scale, size_z, keep, refs[:5], *refs[5:]),
        out_shape=jax.ShapeDtypeStruct((keep, lanes), jnp.float32),
        scratch_shapes=[pltpu.VMEM((2, rows, lanes), jnp.float32)],
        cost_estimate=pl.CostEstimate(
            flops=40 * CSWEEPS * rows * lanes, transcendentals=0, bytes_accessed=24 * rows * lanes
        ),
    )
    return call(*near, lower, upper)


def on_device(pressure_in, source, permeability):
    scales = [0.25**level for level in range(LEVELS + 1)]
    k0, p0, b0 = halo(jnp.stack([permeability, pressure_in, source]), 4)
    lev0 = Level(faces_of(k0, scales[0]), 3, b0, 4)
    p = lev0.sweep(p0, 3)
    s0 = lev0.sweep(p, 2)
    rhs = coarsen(lev0.residual(trim(s0, 1)))
    perm = coarsen(permeability)
    k1, b1 = halo(jnp.stack([perm, rhs]), 5)
    lev1 = Level(faces_of(k1, scales[1]), 4, b1, 5)
    p = lev1.first_sweep(4)
    s1 = lev1.sweep(p, 3)
    rhs = coarsen(lev1.residual(trim(s1, 2)))
    perm = coarsen(perm)
    _, size_y2, size_z2 = rhs.shape
    block = jnp.stack([perm, rhs]).reshape(2, rhs.shape[0], size_y2 * size_z2)
    band = lax.all_gather(block, "col", axis=0, tiled=False)
    k2, b2 = jnp.moveaxis(rows_halo(band, 6, 2), 1, 0)
    ops = lane_band_ops(size_z2)
    lev2 = LaneBand(ops, k2, scales[2], 5, b2, 6)
    p = lev2.first_sweep(5)
    s2 = lev2.sweep(p, 4)
    rhs = band_coarsen(lev2.residual(s2[:, 3:-3]), size_y2, size_z2)
    perm = band_coarsen(band[:, 0], size_y2, size_z2)
    blocks, size_x3, lanes3 = rhs.shape
    pair = jnp.stack([rhs, perm], axis=1)
    pair = jnp.transpose(pair, (1, 2, 0, 3)).reshape(2, size_x3, blocks * lanes3)
    correction = coarse_solve(pair, size_z2 // 2, scales[3])
    correction = jnp.transpose(correction.reshape(-1, blocks, lanes3), (1, 0, 2))
    q = s2 + band_prolong(correction, size_y2, size_z2)
    q = lev2.sweep(q, 3)
    u2 = lev2.sweep(q, 2)
    u2 = jnp.concatenate([u2[-1:], u2, u2[:1]], axis=0)
    col = lax.axis_index("col")
    u2 = lax.dynamic_slice_in_dim(u2, col, 3, axis=0)
    edge = 2 * size_z2
    u2 = jnp.concatenate([u2[0, :, -edge:], u2[1], u2[2, :, :edge]], axis=1)
    u2 = u2.reshape(u2.shape[0], size_y2 + 4, size_z2)
    q = s1 + trim(prolong(u2), 1)
    q = lev1.sweep(q, 2)
    u1 = lev1.sweep(q, 1)
    q = s0 + prolong(u1)
    q = lev0.sweep(q, 1)
    return lev0.sweep(q, 0)


def solution(mesh):
    placed = (P("row", "col", None), P("row", "col", None), P("row", "col", None))
    return jax.shard_map(
        on_device, mesh=mesh, in_specs=placed, out_specs=P("row", "col", None), check_vma=False
    )
```
